32 devices in a mesh: dp: 8 (over z, x), spatial: 4 (over y, core).
Axes of the slice: x: 2, y: 2, z: 4, core: 2. Of those that a mesh axis runs over, the one named last changes fastest.
Arguments:
- fields: bfloat16 [8, 64, 128, 768], P('dp', 'spatial'), may hold values from -6 to 6
- norm_gain: float32 [768], replicated, may hold values from 0.5 to 1.5
- norm_shift: float32 [768], replicated, may hold values from -3 to 3
- first_weight: bfloat16 [2, 8, 96, 96], replicated, may hold values from -0.4375 to 0.4375
- first_bias: float32 [8, 192], replicated, may hold values from -3 to 3
- second_weight: bfloat16 [2, 8, 96, 96], replicated, may hold values from -0.4375 to 0.4375
- second_bias: float32 [8, 192], replicated, may hold values from -3 to 3
- cotangent: bfloat16 [8, 64, 128, 768], P('dp', 'spatial'), may hold values from -6 to 6
Outputs:
- block_output: bfloat16 [8, 64, 128, 768], P('dp', 'spatial')
- grad_fields: bfloat16 [8, 64, 128, 768], P('dp', 'spatial')
- grad_first: float32 [2, 8, 96, 96], replicated
- grad_first_bias: float32 [8, 192], replicated
- grad_second: float32 [2, 8, 96, 96], replicated
- grad_second_bias: float32 [8, 192], replicated
- grad_gain: float32 [768], replicated
- grad_shift: float32 [768], replicated
The draws below stay inside these ranges and needn't reach their ends.
All inputs are finite; a program needn't handle non-finite values.
Results may differ from the reference program's by a relative error of at most 0.017.
The reference program's roundings to bfloat16 on the way count: a program that leaves them out, or rounds other values in their place, can miss the bound.
Values may be sent and summed in bfloat16 or wider, within the bound.
No kernel may reach another device: no remote copies, remote signals or barrier semaphores. Data moves between devices by JAX's collectives and lax.ppermute only.
A program may use at most 192 MiB of HBM per device.

```python
import math
import jax
import jax.numpy as jnp
from jax import lax

LAT = 64
LON = 128
BLOCKS = 8
BLOCK = 96
CHANNELS = 768
MODES = 64
BATCH = 8
TOKENS = 65536


def levels(own_key, dims, split, least, top_value):
    gain = 1.0
    for position, shards_of in split:
        heights = jax.random.uniform(jax.random.fold_in(jax.random.fold_in(own_key, 6), position), (shards_of,), jnp.float32, least / len(split), top_value / len(split))
        gain = gain * jnp.repeat(jnp.exp(heights), dims[position] // shards_of).reshape((-1,) + (1,) * (len(dims) - 1 - position))
    return gain


def normal_values(rng, shape, scale, most, split=(), held_as=jnp.bfloat16):
    values = scale * jax.random.normal(rng, shape, jnp.float32)
    if split:
        values = values * levels(rng, shape, split, -0.22, 0.18)
    return jnp.clip(values, -most, most).astype(held_as)


def setup_inputs(seed: int = 0) -> dict:
    arg_keys = jax.random.split(jax.random.key(seed), 9)
    fields = normal_values(arg_keys[0], (BATCH, LAT, LON, CHANNELS), 1.0, 6.0, ((0, 8), (1, 4)))
    norm_gain = jnp.clip(1.0 + 0.1 * jax.random.normal(arg_keys[1], (CHANNELS,), jnp.float32), 0.5, 1.5)
    norm_shift = normal_values(arg_keys[2], (CHANNELS,), 0.5, 3.0, (), jnp.float32)
    first_weight = normal_values(arg_keys[3], (2, BLOCKS, BLOCK, BLOCK), (2 * BLOCK) ** -0.5, 0.4375)
    first_bias = normal_values(arg_keys[4], (BLOCKS, 2 * BLOCK), 0.5, 3.0, (), jnp.float32)
    second_weight = normal_values(arg_keys[5], (2, BLOCKS, BLOCK, BLOCK), (2 * BLOCK) ** -0.5, 0.4375)
    second_bias = normal_values(arg_keys[6], (BLOCKS, 2 * BLOCK), 0.5, 3.0, (), jnp.float32)
    cotangent = normal_values(arg_keys[7], (BATCH, LAT, LON, CHANNELS), 1.0, 6.0, ((0, 8), (1, 4)))
    return dict(fields=fields, norm_gain=norm_gain, norm_shift=norm_shift, first_weight=first_weight, first_bias=first_bias, second_weight=second_weight, second_bias=second_bias, cotangent=cotangent)


shrink_cut = 0.01
norm_epsilon = 1e-06
gelu_factor = 0.7978845608
gelu_cubic = 0.044715

def product(pattern, left_side, right_side):
    return jnp.einsum(pattern, left_side.astype(jnp.float32), right_side.astype(jnp.float32))

def tables(count, mode_count, doubled):
    positions = jnp.arange(count, dtype=jnp.int32)
    orders = jnp.arange(mode_count, dtype=jnp.int32)
    phases = orders[:, None] * positions[None, :] % count
    angles = 2.0 * math.pi / count * phases.astype(jnp.float32)
    factor = jnp.ones((mode_count, 1), jnp.float32) / math.sqrt(count)
    if doubled:
        factor = factor * jnp.where(orders == 0, 1.0, 2.0).astype(jnp.float32)[:, None]
    return ((jnp.cos(angles) * factor).astype(jnp.bfloat16), (jnp.sin(angles) * factor).astype(jnp.bfloat16))

def rotate(values):
    half_width = values.shape[-1] // 2
    return jnp.concatenate([values[..., half_width:], -values[..., :half_width]], axis=-1)

def along_lon(real_part, cos_table, sin_table):
    real_sum = product('bhwnp,mw->bhmnp', real_part, cos_table)
    imag_sum = -product('bhwnp,mw->bhmnp', real_part, sin_table)
    return jnp.concatenate([real_sum, imag_sum], axis=-1).astype(jnp.bfloat16)

def back_lon(spectral, cos_table, sin_table):
    half_width = spectral.shape[-1] // 2
    return product('bhmnp,mw->bhwnp', spectral[..., :half_width], cos_table) - product('bhmnp,mw->bhwnp', spectral[..., half_width:], sin_table)

def along_lat(spectral, cos_table, sin_table):
    direct = product('kh,bhmnp->bkmnp', cos_table, spectral)
    turned = product('kh,bhmnp->bkmnp', sin_table, spectral)
    return (direct + rotate(turned)).astype(jnp.bfloat16)

def back_lat(spectral, cos_table, sin_table):
    direct = product('kh,bhmnp->bkmnp', cos_table, spectral)
    turned = product('kh,bhmnp->bkmnp', sin_table, spectral)
    return (direct - rotate(turned)).astype(jnp.bfloat16)

def real_blocks(weight):
    upper_rows = jnp.concatenate([weight[0], weight[1]], axis=-1)
    bottom = jnp.concatenate([-weight[1], weight[0]], axis=-1)
    return jnp.concatenate([upper_rows, bottom], axis=1)

def fold_blocks(gradient):
    half_width = gradient.shape[-1] // 2
    real_grad = gradient[:, :half_width, :half_width] + gradient[:, half_width:, half_width:]
    imag_grad = gradient[:, :half_width, half_width:] - gradient[:, half_width:, :half_width]
    return jnp.stack([real_grad, imag_grad])

def gelu_value(values):
    inner = jnp.tanh(gelu_factor * (values + gelu_cubic * values * values * values))
    return 0.5 * values * (1.0 + inner)

def gelu_slope(values):
    inner = jnp.tanh(gelu_factor * (values + gelu_cubic * values * values * values))
    return 0.5 * (1.0 + inner) + 0.5 * values * (1.0 - inner * inner) * gelu_factor * (1.0 + 3.0 * gelu_cubic * values * values)

def spectral_forward(transformed, first_real, first_bias, second_real, second_bias):
    hidden_pre = product('bkmnp,npq->bkmnq', transformed, first_real) + first_bias
    hidden = gelu_value(hidden_pre).astype(jnp.bfloat16)
    output_pre = product('bkmnp,npq->bkmnq', hidden, second_real) + second_bias
    shrunk = (output_pre - shrink_cut * jnp.tanh(output_pre / shrink_cut)).astype(jnp.bfloat16)
    return (hidden_pre, hidden, output_pre, shrunk)

def spectral_backward(transformed, hidden_pre, hidden, output_pre, grad_shrunk, first_real, second_real):
    bend = jnp.tanh(output_pre / shrink_cut)
    grad_outpre = (grad_shrunk.astype(jnp.float32) * bend * bend).astype(jnp.bfloat16)
    grad_second = product('bkmnp,bkmnq->npq', hidden, grad_outpre)
    grad_second_bias = lax.optimization_barrier(jnp.sum(grad_outpre.astype(jnp.float32), axis=(0, 1, 2)))
    grad_hidden = product('bkmnq,npq->bkmnp', grad_outpre, second_real)
    grad_hidpre = (grad_hidden * gelu_slope(hidden_pre)).astype(jnp.bfloat16)
    grad_first = product('bkmnp,bkmnq->npq', transformed, grad_hidpre)
    grad_first_bias = lax.optimization_barrier(jnp.sum(grad_hidpre.astype(jnp.float32), axis=(0, 1, 2)))
    grad_transformed = product('bkmnq,npq->bkmnp', grad_hidpre, first_real).astype(jnp.bfloat16)
    return (grad_transformed, grad_first, grad_first_bias, grad_second, grad_second_bias)

def normalize(fields):
    values = fields.astype(jnp.float32)
    center = lax.optimization_barrier(jnp.mean(values, axis=-1, keepdims=True))
    spread = lax.optimization_barrier(jnp.mean((values - center) ** 2, axis=-1, keepdims=True))
    inverse_std = lax.rsqrt(spread + norm_epsilon)
    return ((values - center) * inverse_std, inverse_std)

def norm_backward(grad_scaled, normed, inverse_std, norm_gain):
    grad_normed = grad_scaled * norm_gain
    mean_grad = lax.optimization_barrier(jnp.mean(grad_normed, axis=-1, keepdims=True))
    mean_cross = lax.optimization_barrier(jnp.mean(grad_normed * normed, axis=-1, keepdims=True))
    return inverse_std * (grad_normed - mean_grad - normed * mean_cross)

def reference(fields, norm_gain, norm_shift, first_weight, first_bias, second_weight, second_bias, cotangent):
    ahead_cos, ahead_sin = tables(LON, MODES, False)
    back_cos, back_sin = tables(LON, MODES, True)
    polar_cos, polar_sin = tables(LAT, LAT, False)
    first_real = real_blocks(first_weight)
    second_real = real_blocks(second_weight)

    def advance(carry, sample):
        sample_fields, sample_cot = sample
        sample_fields = sample_fields[None]
        sample_cot = sample_cot[None]
        block_shape = (1, LAT, LON, BLOCKS, BLOCK)
        normed, inverse_std = normalize(sample_fields)
        scaled = (normed * norm_gain + norm_shift).astype(jnp.bfloat16)
        spectral = along_lon(scaled.reshape(block_shape), ahead_cos, ahead_sin)
        transformed = along_lat(spectral, polar_cos, polar_sin)
        hidden_pre, hidden, output_pre, shrunk = spectral_forward(transformed, first_real, first_bias, second_real, second_bias)
        returned = back_lat(shrunk, polar_cos, polar_sin)
        mixed = back_lon(returned, back_cos, back_sin).reshape(sample_fields.shape)
        output = (sample_fields.astype(jnp.float32) + scaled.astype(jnp.float32) + mixed).astype(jnp.bfloat16)
        grad_returned = along_lon(sample_cot.reshape(block_shape), back_cos, back_sin)
        grad_shrunk = along_lat(grad_returned, polar_cos, polar_sin)
        grad_transformed, g_first, g_first_bias, g_second, g_second_bias = spectral_backward(transformed, hidden_pre, hidden, output_pre, grad_shrunk, first_real, second_real)
        grad_spectral = back_lat(grad_transformed, polar_cos, polar_sin)
        grad_scaled = sample_cot.astype(jnp.float32) + back_lon(grad_spectral, ahead_cos, ahead_sin).reshape(sample_fields.shape)
        grad_out = (sample_cot.astype(jnp.float32) + norm_backward(grad_scaled, normed, inverse_std, norm_gain)).astype(jnp.bfloat16)
        g_gain = lax.optimization_barrier(jnp.sum(grad_scaled * normed, axis=(0, 1, 2)))
        g_shift = lax.optimization_barrier(jnp.sum(grad_scaled, axis=(0, 1, 2)))
        terms = (g_first, g_first_bias, g_second, g_second_bias, g_gain, g_shift)
        carry = tuple((total + term for total, term in zip(carry, terms)))
        return (carry, (output[0], grad_out[0]))
    width = 2 * BLOCK
    start = (jnp.zeros((BLOCKS, width, width), jnp.float32), jnp.zeros((BLOCKS, width), jnp.float32), jnp.zeros((BLOCKS, width, width), jnp.float32), jnp.zeros((BLOCKS, width), jnp.float32), jnp.zeros((CHANNELS,), jnp.float32), jnp.zeros((CHANNELS,), jnp.float32))
    totals, outputs = lax.scan(advance, start, (fields, cotangent))
    scale = 1.0 / math.sqrt(TOKENS)
    return (outputs[0], outputs[1], fold_blocks(totals[0]) * scale, totals[1] * scale, fold_blocks(totals[2]) * scale, totals[3] * scale, totals[4] * scale, totals[5] * scale)
```

```python
import math

import jax
import jax.numpy as jnp
from jax import lax
from jax.sharding import PartitionSpec as P

LAT = 64
LON = 128
BLOCKS = 8
BLOCK = 96


shrink_cut = 0.01
norm_epsilon = 1e-06
gelu_factor = 0.7978845608
gelu_cubic = 0.044715


def product(pattern, left_side, right_side):
    return jnp.einsum(pattern, left_side, right_side, preferred_element_type=jnp.float32)


def tables(count, mode_count, doubled):
    positions = jnp.arange(count, dtype=jnp.int32)
    orders = jnp.arange(mode_count, dtype=jnp.int32)
    phases = orders[:, None] * positions[None, :] % count
    angles = 2.0 * math.pi / count * phases.astype(jnp.float32)
    factor = jnp.ones((mode_count, 1), jnp.float32) / math.sqrt(count)
    if doubled:
        factor = factor * jnp.where(orders == 0, 1.0, 2.0).astype(jnp.float32)[:, None]
    return (
        (jnp.cos(angles) * factor).astype(jnp.bfloat16),
        (jnp.sin(angles) * factor).astype(jnp.bfloat16),
    )


def rotate(values):
    half_width = values.shape[-1] // 2
    return jnp.concatenate([values[..., half_width:], -values[..., :half_width]], axis=-1)


def along_lon(real_part, cos_table, sin_table):
    real_sum = product("bhwnp,mw->bhmnp", real_part, cos_table)
    imag_sum = -product("bhwnp,mw->bhmnp", real_part, sin_table)
    return jnp.concatenate([real_sum, imag_sum], axis=-1).astype(jnp.bfloat16)


def back_lon(spectral, cos_table, sin_table):
    half_width = spectral.shape[-1] // 2
    return product("bhmnp,mw->bhwnp", spectral[..., :half_width], cos_table) - product(
        "bhmnp,mw->bhwnp", spectral[..., half_width:], sin_table
    )


def along_lat(spectral, cos_table, sin_table):
    direct = product("kh,bhmnp->bkmnp", cos_table, spectral)
    turned = product("kh,bhmnp->bkmnp", sin_table, spectral)
    return (direct + rotate(turned)).astype(jnp.bfloat16)


def back_lat(spectral, cos_table, sin_table):
    direct = product("kh,bhmnp->bkmnp", cos_table, spectral)
    turned = product("kh,bhmnp->bkmnp", sin_table, spectral)
    return (direct - rotate(turned)).astype(jnp.bfloat16)


def real_blocks(weight):
    upper_rows = jnp.concatenate([weight[0], weight[1]], axis=-1)
    bottom = jnp.concatenate([-weight[1], weight[0]], axis=-1)
    return jnp.concatenate([upper_rows, bottom], axis=1)


def fold_blocks(gradient):
    half_width = gradient.shape[-1] // 2
    real_grad = gradient[:, :half_width, :half_width] + gradient[:, half_width:, half_width:]
    imag_grad = gradient[:, :half_width, half_width:] - gradient[:, half_width:, :half_width]
    return jnp.stack([real_grad, imag_grad])


def gelu_value(values):
    inner = jnp.tanh(gelu_factor * (values + gelu_cubic * values * values * values))
    return 0.5 * values * (1.0 + inner)


def gelu_slope(values):
    inner = jnp.tanh(gelu_factor * (values + gelu_cubic * values * values * values))
    return 0.5 * (1.0 + inner) + 0.5 * values * (1.0 - inner * inner) * gelu_factor * (
        1.0 + 3.0 * gelu_cubic * values * values
    )


def spectral_forward(transformed, first_real, first_bias, second_real, second_bias):
    hidden_pre = product("bkmnp,npq->bkmnq", transformed, first_real) + first_bias
    hidden = gelu_value(hidden_pre).astype(jnp.bfloat16)
    output_pre = product("bkmnp,npq->bkmnq", hidden, second_real) + second_bias
    shrunk = (output_pre - shrink_cut * jnp.tanh(output_pre / shrink_cut)).astype(jnp.bfloat16)
    return (hidden_pre, hidden, output_pre, shrunk)


def spectral_backward(
    transformed, hidden_pre, hidden, output_pre, grad_shrunk, first_real, second_real
):
    bend = jnp.tanh(output_pre / shrink_cut)
    grad_outpre = (grad_shrunk.astype(jnp.float32) * bend * bend).astype(jnp.bfloat16)
    grad_second = product("bkmnp,bkmnq->npq", hidden, grad_outpre)
    grad_second_bias = jnp.sum(grad_outpre.astype(jnp.float32), axis=(0, 1, 2))
    grad_hidden = product("bkmnq,npq->bkmnp", grad_outpre, second_real)
    grad_hidpre = (grad_hidden * gelu_slope(hidden_pre)).astype(jnp.bfloat16)
    grad_first = product("bkmnp,bkmnq->npq", transformed, grad_hidpre)
    grad_first_bias = jnp.sum(grad_hidpre.astype(jnp.float32), axis=(0, 1, 2))
    grad_transformed = product("bkmnq,npq->bkmnp", grad_hidpre, first_real).astype(jnp.bfloat16)
    return (grad_transformed, grad_first, grad_first_bias, grad_second, grad_second_bias)


def normalize(fields):
    values = fields.astype(jnp.float32)
    center = jnp.mean(values, axis=-1, keepdims=True)
    spread = jnp.mean((values - center) ** 2, axis=-1, keepdims=True)
    inverse_std = lax.rsqrt(spread + norm_epsilon)
    return ((values - center) * inverse_std, inverse_std)


def norm_backward(grad_scaled, normed, inverse_std, norm_gain):
    grad_normed = grad_scaled * norm_gain
    mean_grad = jnp.mean(grad_normed, axis=-1, keepdims=True)
    mean_cross = jnp.mean(grad_normed * normed, axis=-1, keepdims=True)
    return inverse_std * (grad_normed - mean_grad - normed * mean_cross)


def local(
    fields, norm_gain, norm_shift, first_weight, first_bias, second_weight, second_bias, cotangent
):
    samples, band_rows, longitudes, channels = fields.shape
    mode_count = longitudes // 2
    ahead_cos, ahead_sin = tables(longitudes, mode_count, False)
    back_cos, back_sin = tables(longitudes, mode_count, True)
    polar_cos, polar_sin = tables(LAT, LAT, False)
    first_real = real_blocks(first_weight)
    second_real = real_blocks(second_weight)
    block_shape = (samples, band_rows, longitudes, BLOCKS, BLOCK)
    normed, inverse_std = normalize(fields)
    scaled = (normed * norm_gain + norm_shift).astype(jnp.bfloat16)
    spectral = along_lon(scaled.reshape(block_shape), ahead_cos, ahead_sin)
    grad_returned = along_lon(cotangent.reshape(block_shape), back_cos, back_sin)
    columns = lax.all_to_all(spectral, "spatial", split_axis=2, concat_axis=1, tiled=True)
    transformed = along_lat(columns, polar_cos, polar_sin)
    hidden_pre, hidden, output_pre, shrunk = spectral_forward(
        transformed, first_real, first_bias, second_real, second_bias
    )
    returned = back_lat(shrunk, polar_cos, polar_sin)
    banded = lax.all_to_all(returned, "spatial", split_axis=1, concat_axis=2, tiled=True)
    mixed = back_lon(banded, back_cos, back_sin).reshape(fields.shape)
    block_output = (fields.astype(jnp.float32) + scaled.astype(jnp.float32) + mixed).astype(
        jnp.bfloat16
    )
    grad_columns = lax.all_to_all(grad_returned, "spatial", split_axis=2, concat_axis=1, tiled=True)
    grad_shrunk = along_lat(grad_columns, polar_cos, polar_sin)
    grad_transformed, g_first, g_first_bias, g_second, g_second_bias = spectral_backward(
        transformed, hidden_pre, hidden, output_pre, grad_shrunk, first_real, second_real
    )
    grad_spectral = back_lat(grad_transformed, polar_cos, polar_sin)
    grad_banded = lax.all_to_all(grad_spectral, "spatial", split_axis=1, concat_axis=2, tiled=True)
    grad_scaled = cotangent.astype(jnp.float32) + back_lon(
        grad_banded, ahead_cos, ahead_sin
    ).reshape(fields.shape)
    grad_fields = (
        cotangent.astype(jnp.float32) + norm_backward(grad_scaled, normed, inverse_std, norm_gain)
    ).astype(jnp.bfloat16)
    g_gain = jnp.sum(grad_scaled * normed, axis=(0, 1, 2))
    g_shift = jnp.sum(grad_scaled, axis=(0, 1, 2))
    token_total = lax.axis_size("dp") * samples * LAT * LON
    scale = 1.0 / math.sqrt(token_total)
    early = psum_flat((fold_blocks(g_first), g_first_bias, fold_blocks(g_second), g_second_bias))
    late = psum_flat((g_gain, g_shift))
    return (block_output, grad_fields) + tuple(part * scale for part in early + late)


def psum_flat(parts):
    flat = jnp.concatenate([part.reshape(-1) for part in parts])
    size = flat.shape[0]
    padded = -(-size // 1024) * 1024
    flat = jnp.pad(flat, (0, padded - size)).reshape(padded // 128, 128)
    flat = lax.psum(flat, ("dp", "spatial")).reshape(-1)
    pieces, offset = [], 0
    for part in parts:
        pieces.append(flat[offset : offset + part.size].reshape(part.shape))
        offset += part.size
    return tuple(pieces)


def solution(mesh):
    return jax.shard_map(
        local,
        mesh=mesh,
        in_specs=(
            P("dp", "spatial", None, None),
            P(),
            P(),
            P(),
            P(),
            P(),
            P(),
            P("dp", "spatial", None, None),
        ),
        out_specs=(
            P("dp", "spatial", None, None),
            P("dp", "spatial", None, None),
            P(),
            P(),
            P(),
            P(),
            P(),
            P(),
        ),
        check_vma=False,
    )
```

```python
import math

import jax
import jax.numpy as jnp
from jax import lax
from jax.sharding import PartitionSpec as P


LAT = 64
LON = 128
BLOCKS = 8
BLOCK = 96


shrink_cut = 0.01
norm_epsilon = 1e-06
gelu_factor = 0.7978845608
gelu_cubic = 0.044715


def product(pattern, left_side, right_side):
    return jnp.einsum(pattern, left_side, right_side, preferred_element_type=jnp.float32)


def tables(count, mode_count, doubled):
    positions = jnp.arange(count, dtype=jnp.int32)
    orders = jnp.arange(mode_count, dtype=jnp.int32)
    phases = orders[:, None] * positions[None, :] % count
    angles = 2.0 * math.pi / count * phases.astype(jnp.float32)
    factor = jnp.ones((mode_count, 1), jnp.float32) / math.sqrt(count)
    if doubled:
        factor = factor * jnp.where(orders == 0, 1.0, 2.0).astype(jnp.float32)[:, None]
    return (
        (jnp.cos(angles) * factor).astype(jnp.bfloat16),
        (jnp.sin(angles) * factor).astype(jnp.bfloat16),
    )


def rotate(values):
    half_width = values.shape[-1] // 2
    return jnp.concatenate([values[..., half_width:], -values[..., :half_width]], axis=-1)


def along_lon(real_part, cos_table, sin_table):
    real_sum = product("bhwnp,mw->bhmnp", real_part, cos_table)
    imag_sum = -product("bhwnp,mw->bhmnp", real_part, sin_table)
    return jnp.concatenate([real_sum, imag_sum], axis=-1).astype(jnp.bfloat16)


def back_lon(spectral, cos_table, sin_table):
    half_width = spectral.shape[-1] // 2
    return product("bhmnp,mw->bhwnp", spectral[..., :half_width], cos_table) - product(
        "bhmnp,mw->bhwnp", spectral[..., half_width:], sin_table
    )


def along_lat(spectral, cos_table, sin_table):
    direct = product("kh,bhmnp->bkmnp", cos_table, spectral)
    turned = product("kh,bhmnp->bkmnp", sin_table, spectral)
    return (direct + rotate(turned)).astype(jnp.bfloat16)


def back_lat(spectral, cos_table, sin_table):
    direct = product("kh,bhmnp->bkmnp", cos_table, spectral)
    turned = product("kh,bhmnp->bkmnp", sin_table, spectral)
    return (direct - rotate(turned)).astype(jnp.bfloat16)


def real_blocks(weight):
    upper_rows = jnp.concatenate([weight[0], weight[1]], axis=-1)
    bottom = jnp.concatenate([-weight[1], weight[0]], axis=-1)
    return jnp.concatenate([upper_rows, bottom], axis=1)


def fold_blocks(gradient):
    half_width = gradient.shape[-1] // 2
    real_grad = gradient[:, :half_width, :half_width] + gradient[:, half_width:, half_width:]
    imag_grad = gradient[:, :half_width, half_width:] - gradient[:, half_width:, :half_width]
    return jnp.stack([real_grad, imag_grad])


def gelu_value(values):
    inner = jnp.tanh(gelu_factor * (values + gelu_cubic * values * values * values))
    return 0.5 * values * (1.0 + inner)


def gelu_slope(values):
    inner = jnp.tanh(gelu_factor * (values + gelu_cubic * values * values * values))
    return 0.5 * (1.0 + inner) + 0.5 * values * (1.0 - inner * inner) * gelu_factor * (
        1.0 + 3.0 * gelu_cubic * values * values
    )


def spectral_forward(transformed, first_real, first_bias, second_real, second_bias):
    hidden_pre = product("bkmnp,npq->bkmnq", transformed, first_real) + first_bias
    hidden = gelu_value(hidden_pre).astype(jnp.bfloat16)
    output_pre = product("bkmnp,npq->bkmnq", hidden, second_real) + second_bias
    shrunk = (output_pre - shrink_cut * jnp.tanh(output_pre / shrink_cut)).astype(jnp.bfloat16)
    return (hidden_pre, hidden, output_pre, shrunk)


def spectral_backward(
    transformed, hidden_pre, hidden, output_pre, grad_shrunk, first_real, second_real
):
    bend = jnp.tanh(output_pre / shrink_cut)
    grad_outpre = (grad_shrunk.astype(jnp.float32) * bend * bend).astype(jnp.bfloat16)
    grad_second = product("bkmnp,bkmnq->npq", hidden, grad_outpre)
    grad_second_bias = jnp.sum(grad_outpre.astype(jnp.float32), axis=(0, 1, 2))
    grad_hidden = product("bkmnq,npq->bkmnp", grad_outpre, second_real)
    grad_hidpre = (grad_hidden * gelu_slope(hidden_pre)).astype(jnp.bfloat16)
    grad_first = product("bkmnp,bkmnq->npq", transformed, grad_hidpre)
    grad_first_bias = jnp.sum(grad_hidpre.astype(jnp.float32), axis=(0, 1, 2))
    grad_transformed = product("bkmnq,npq->bkmnp", grad_hidpre, first_real).astype(jnp.bfloat16)
    return (grad_transformed, grad_first, grad_first_bias, grad_second, grad_second_bias)


def normalize(fields):
    values = fields.astype(jnp.float32)
    center = jnp.mean(values, axis=-1, keepdims=True)
    spread = jnp.mean((values - center) ** 2, axis=-1, keepdims=True)
    inverse_std = lax.rsqrt(spread + norm_epsilon)
    return ((values - center) * inverse_std, inverse_std)


def norm_backward(grad_scaled, normed, inverse_std, norm_gain):
    grad_normed = grad_scaled * norm_gain
    mean_grad = jnp.mean(grad_normed, axis=-1, keepdims=True)
    mean_cross = jnp.mean(grad_normed * normed, axis=-1, keepdims=True)
    return inverse_std * (grad_normed - mean_grad - normed * mean_cross)


def send_order(me, n, size):
    chunk = (me + jnp.arange(n, dtype=jnp.int32)[:, None]) % n
    return (chunk * size + jnp.arange(size, dtype=jnp.int32)[None, :]).reshape(-1)


def receive_order(me, n, size):
    chunk = (me + n - jnp.arange(n, dtype=jnp.int32)[:, None]) % n
    return (chunk * size + jnp.arange(size, dtype=jnp.int32)[None, :]).reshape(-1)


def exchange(values, split_axis, concat_axis):
    n = lax.axis_size("spatial")
    size = values.shape[split_axis] // n
    pieces = [lax.slice_in_dim(values, k * size, (k + 1) * size, axis=split_axis) for k in range(n)]
    received = [pieces[0]] + [
        lax.ppermute(pieces[k], "spatial", [(i, (i + k) % n) for i in range(n)])
        for k in range(1, n)
    ]
    return jnp.concatenate(received, axis=concat_axis)


def allsum_small(values):
    for axis in ("spatial", "dp"):
        n = lax.axis_size(axis)
        if n & (n - 1):
            values = lax.psum(values, axis)
            continue
        step = 1
        while step < n:
            values = values + lax.ppermute(values, axis, [(i, i ^ step) for i in range(n)])
            step *= 2
    return values


def local(
    fields, norm_gain, norm_shift, first_weight, first_bias, second_weight, second_bias, cotangent
):
  samples, band_rows, longitudes, _ = fields.shape
  mode_count = longitudes // 2
  n = lax.axis_size("spatial")
  me = lax.axis_index("spatial")
  modes_per = mode_count // n
  send_m = send_order(me, n, modes_per)
  recv_m = receive_order(me, n, modes_per)
  send_h = send_order(me, n, band_rows)
  recv_h = receive_order(me, n, band_rows)
  ahead_cos, ahead_sin = tables(longitudes, mode_count, False)
  back_cos, back_sin = tables(longitudes, mode_count, True)
  polar_cos, polar_sin = tables(LAT, LAT, False)
  first_real = real_blocks(first_weight)
  second_real = real_blocks(second_weight)
  block_shape = (samples, band_rows, longitudes, BLOCKS, BLOCK)
  normed, inverse_std = normalize(fields)
  scaled = (normed * norm_gain + norm_shift).astype(jnp.bfloat16)
  spectral = along_lon(scaled.reshape(block_shape), ahead_cos[send_m], ahead_sin[send_m])
  columns = exchange(spectral, 2, 1)
  grad_returned = along_lon(cotangent.reshape(block_shape), back_cos[send_m], back_sin[send_m])
  grad_columns = exchange(grad_returned, 2, 1)
  transformed = along_lat(columns, polar_cos[:, recv_h], polar_sin[:, recv_h])
  hidden_pre, hidden, output_pre, shrunk = spectral_forward(
      transformed, first_real, first_bias, second_real, second_bias
  )
  returned = back_lat(shrunk, polar_cos[send_h], polar_sin[send_h])
  banded = exchange(returned, 1, 2)
  grad_shrunk = along_lat(grad_columns, polar_cos[:, recv_h], polar_sin[:, recv_h])
  grad_transformed, g_first, g_first_bias, g_second, g_second_bias = spectral_backward(
      transformed, hidden_pre, hidden, output_pre, grad_shrunk, first_real, second_real
  )
  grad_spectral = back_lat(grad_transformed, polar_cos[send_h], polar_sin[send_h])
  grad_banded = exchange(grad_spectral, 1, 2)
  early = psum_flat((fold_blocks(g_first), g_first_bias, fold_blocks(g_second), g_second_bias))
  mixed = back_lon(banded, back_cos[recv_m], back_sin[recv_m]).reshape(fields.shape)
  block_output = (fields.astype(jnp.float32) + scaled.astype(jnp.float32) + mixed).astype(
      jnp.bfloat16
  )
  grad_scaled = cotangent.astype(jnp.float32) + back_lon(
      grad_banded, ahead_cos[recv_m], ahead_sin[recv_m]
  ).reshape(fields.shape)
  grad_fields = (
      cotangent.astype(jnp.float32) + norm_backward(grad_scaled, normed, inverse_std, norm_gain)
  ).astype(jnp.bfloat16)
  g_gain = jnp.sum(grad_scaled * normed, axis=(0, 1, 2))
  g_shift = jnp.sum(grad_scaled, axis=(0, 1, 2))
  late = allsum_small(jnp.stack([g_gain, g_shift]))
  token_total = lax.axis_size("dp") * samples * LAT * LON
  scale = 1.0 / math.sqrt(token_total)
  return (block_output, grad_fields) + tuple(part * scale for part in early) + (
      late[0] * scale,
      late[1] * scale,
  )


def psum_flat(parts):
    flat = jnp.concatenate([part.reshape(-1) for part in parts])
    size = flat.shape[0]
    padded = -(-size // 1024) * 1024
    flat = jnp.pad(flat, (0, padded - size)).reshape(padded // 128, 128)
    flat = lax.psum(flat, ("dp", "spatial")).reshape(-1)
    pieces, offset = [], 0
    for part in parts:
        pieces.append(flat[offset : offset + part.size].reshape(part.shape))
        offset += part.size
    return tuple(pieces)


def solution(mesh):
    return jax.shard_map(
        local,
        mesh=mesh,
        in_specs=(
            P("dp", "spatial", None, None),
            P(),
            P(),
            P(),
            P(),
            P(),
            P(),
            P("dp", "spatial", None, None),
        ),
        out_specs=(
            P("dp", "spatial", None, None),
            P("dp", "spatial", None, None),
            P(),
            P(),
            P(),
            P(),
            P(),
            P(),
        ),
        check_vma=False,
    )
```

```python
import math

import jax
import jax.numpy as jnp
from jax import lax
from jax.sharding import PartitionSpec as P


LAT = 64
LON = 128
BLOCKS = 8
BLOCK = 96


shrink_cut = 0.01
norm_epsilon = 1e-06
gelu_factor = 0.7978845608
gelu_cubic = 0.044715


def product(pattern, left_side, right_side):
    return jnp.einsum(pattern, left_side, right_side, preferred_element_type=jnp.float32)


def tables(count, mode_count, doubled):
    positions = jnp.arange(count, dtype=jnp.int32)
    orders = jnp.arange(mode_count, dtype=jnp.int32)
    phases = orders[:, None] * positions[None, :] % count
    angles = 2.0 * math.pi / count * phases.astype(jnp.float32)
    factor = jnp.ones((mode_count, 1), jnp.float32) / math.sqrt(count)
    if doubled:
        factor = factor * jnp.where(orders == 0, 1.0, 2.0).astype(jnp.float32)[:, None]
    return (
        (jnp.cos(angles) * factor).astype(jnp.bfloat16),
        (jnp.sin(angles) * factor).astype(jnp.bfloat16),
    )


def rotate(values):
    half_width = values.shape[-1] // 2
    return jnp.concatenate([values[..., half_width:], -values[..., :half_width]], axis=-1)


def along_lon(real_part, cos_table, sin_table):
    real_sum = product("bhwnp,mw->bhmnp", real_part, cos_table)
    imag_sum = -product("bhwnp,mw->bhmnp", real_part, sin_table)
    return jnp.concatenate([real_sum, imag_sum], axis=-1).astype(jnp.bfloat16)


def back_lon(spectral, cos_table, sin_table):
    half_width = spectral.shape[-1] // 2
    return product("bhmnp,mw->bhwnp", spectral[..., :half_width], cos_table) - product(
        "bhmnp,mw->bhwnp", spectral[..., half_width:], sin_table
    )


def along_lat(spectral, cos_table, sin_table):
    stacked = jnp.concatenate([spectral, rotate(spectral)], axis=1)
    table = jnp.concatenate([cos_table, sin_table], axis=1)
    return product("kh,bhmnp->bkmnp", table, stacked).astype(jnp.bfloat16)


def back_lat(spectral, cos_table, sin_table):
    stacked = jnp.concatenate([spectral, -rotate(spectral)], axis=1)
    table = jnp.concatenate([cos_table, sin_table], axis=1)
    return product("kh,bhmnp->bkmnp", table, stacked).astype(jnp.bfloat16)


def real_blocks(weight):
    upper_rows = jnp.concatenate([weight[0], weight[1]], axis=-1)
    bottom = jnp.concatenate([-weight[1], weight[0]], axis=-1)
    return jnp.concatenate([upper_rows, bottom], axis=1)


def fold_blocks(gradient):
    half_width = gradient.shape[-1] // 2
    real_grad = gradient[:, :half_width, :half_width] + gradient[:, half_width:, half_width:]
    imag_grad = gradient[:, :half_width, half_width:] - gradient[:, half_width:, :half_width]
    return jnp.stack([real_grad, imag_grad])


def gelu_value(values):
    inner = jnp.tanh(gelu_factor * (values + gelu_cubic * values * values * values))
    return 0.5 * values * (1.0 + inner)


def gelu_slope(values):
    inner = jnp.tanh(gelu_factor * (values + gelu_cubic * values * values * values))
    return 0.5 * (1.0 + inner) + 0.5 * values * (1.0 - inner * inner) * gelu_factor * (
        1.0 + 3.0 * gelu_cubic * values * values
    )


def spectral_forward(transformed, first_real, first_bias, second_real, second_bias):
    hidden_pre = product("bkmnp,npq->bkmnq", transformed, first_real) + first_bias
    hidden = gelu_value(hidden_pre).astype(jnp.bfloat16)
    output_pre = product("bkmnp,npq->bkmnq", hidden, second_real) + second_bias
    shrunk = (output_pre - shrink_cut * jnp.tanh(output_pre / shrink_cut)).astype(jnp.bfloat16)
    return (hidden_pre, hidden, output_pre, shrunk)


def spectral_backward(
    transformed, hidden_pre, hidden, output_pre, grad_shrunk, first_real, second_real
):
    bend = jnp.tanh(output_pre / shrink_cut)
    grad_outpre = (grad_shrunk.astype(jnp.float32) * bend * bend).astype(jnp.bfloat16)
    grad_second = product("bkmnp,bkmnq->npq", hidden, grad_outpre)
    grad_second_bias = jnp.sum(grad_outpre.astype(jnp.float32), axis=(0, 1, 2))
    grad_hidden = product("bkmnq,npq->bkmnp", grad_outpre, second_real)
    grad_hidpre = (grad_hidden * gelu_slope(hidden_pre)).astype(jnp.bfloat16)
    grad_first = product("bkmnp,bkmnq->npq", transformed, grad_hidpre)
    grad_first_bias = jnp.sum(grad_hidpre.astype(jnp.float32), axis=(0, 1, 2))
    grad_transformed = product("bkmnq,npq->bkmnp", grad_hidpre, first_real).astype(jnp.bfloat16)
    return (grad_transformed, grad_first, grad_first_bias, grad_second, grad_second_bias)


def normalize(fields):
    values = fields.astype(jnp.float32)
    center = jnp.mean(values, axis=-1, keepdims=True)
    spread = jnp.mean((values - center) ** 2, axis=-1, keepdims=True)
    inverse_std = lax.rsqrt(spread + norm_epsilon)
    return ((values - center) * inverse_std, inverse_std)


def norm_backward(grad_scaled, normed, inverse_std, norm_gain):
    grad_normed = grad_scaled * norm_gain
    mean_grad = jnp.mean(grad_normed, axis=-1, keepdims=True)
    mean_cross = jnp.mean(grad_normed * normed, axis=-1, keepdims=True)
    return inverse_std * (grad_normed - mean_grad - normed * mean_cross)


def send_order(me, n, size):
    chunk = (me + jnp.arange(n, dtype=jnp.int32)[:, None]) % n
    return (chunk * size + jnp.arange(size, dtype=jnp.int32)[None, :]).reshape(-1)


def receive_order(me, n, size):
    chunk = (me + n - jnp.arange(n, dtype=jnp.int32)[:, None]) % n
    return (chunk * size + jnp.arange(size, dtype=jnp.int32)[None, :]).reshape(-1)


def exchange(values, split_axis, concat_axis):
    n = lax.axis_size("spatial")
    size = values.shape[split_axis] // n
    pieces = [lax.slice_in_dim(values, k * size, (k + 1) * size, axis=split_axis) for k in range(n)]
    received = [pieces[0]] + [
        lax.ppermute(pieces[k], "spatial", [(i, (i + k) % n) for i in range(n)])
        for k in range(1, n)
    ]
    return jnp.concatenate(received, axis=concat_axis)


def allsum_small(values):
    for axis in ("spatial", "dp"):
        n = lax.axis_size(axis)
        if n & (n - 1):
            values = lax.psum(values, axis)
            continue
        step = 1
        while step < n:
            values = values + lax.ppermute(values, axis, [(i, i ^ step) for i in range(n)])
            step *= 2
    return values


def local(
    fields, norm_gain, norm_shift, first_weight, first_bias, second_weight, second_bias, cotangent
):
  samples, band_rows, longitudes, _ = fields.shape
  mode_count = longitudes // 2
  n = lax.axis_size("spatial")
  me = lax.axis_index("spatial")
  modes_per = mode_count // n
  send_m = send_order(me, n, modes_per)
  recv_m = receive_order(me, n, modes_per)
  send_h = send_order(me, n, band_rows)
  recv_h = receive_order(me, n, band_rows)
  ahead_cos, ahead_sin = tables(longitudes, mode_count, False)
  back_cos, back_sin = tables(longitudes, mode_count, True)
  polar_cos, polar_sin = tables(LAT, LAT, False)
  first_real = real_blocks(first_weight)
  second_real = real_blocks(second_weight)
  block_shape = (samples, band_rows, longitudes, BLOCKS, BLOCK)
  normed, inverse_std = normalize(fields)
  scaled = (normed * norm_gain + norm_shift).astype(jnp.bfloat16)
  spectral = along_lon(scaled.reshape(block_shape), ahead_cos[send_m], ahead_sin[send_m])
  columns = exchange(spectral, 2, 1)
  grad_returned = along_lon(cotangent.reshape(block_shape), back_cos[send_m], back_sin[send_m])
  grad_columns = exchange(grad_returned, 2, 1)
  transformed = along_lat(columns, polar_cos[:, recv_h], polar_sin[:, recv_h])
  hidden_pre, hidden, output_pre, shrunk = spectral_forward(
      transformed, first_real, first_bias, second_real, second_bias
  )
  returned = back_lat(shrunk, polar_cos[send_h], polar_sin[send_h])
  banded = exchange(returned, 1, 2)
  grad_shrunk = along_lat(grad_columns, polar_cos[:, recv_h], polar_sin[:, recv_h])
  grad_transformed, g_first, g_first_bias, g_second, g_second_bias = spectral_backward(
      transformed, hidden_pre, hidden, output_pre, grad_shrunk, first_real, second_real
  )
  grad_spectral = back_lat(grad_transformed, polar_cos[send_h], polar_sin[send_h])
  grad_banded = exchange(grad_spectral, 1, 2)
  early = psum_flat((fold_blocks(g_first), g_first_bias, fold_blocks(g_second), g_second_bias))
  mixed = back_lon(banded, back_cos[recv_m], back_sin[recv_m]).reshape(fields.shape)
  block_output = (fields.astype(jnp.float32) + scaled.astype(jnp.float32) + mixed).astype(
      jnp.bfloat16
  )
  grad_scaled = cotangent.astype(jnp.float32) + back_lon(
      grad_banded, ahead_cos[recv_m], ahead_sin[recv_m]
  ).reshape(fields.shape)
  grad_fields = (
      cotangent.astype(jnp.float32) + norm_backward(grad_scaled, normed, inverse_std, norm_gain)
  ).astype(jnp.bfloat16)
  g_gain = jnp.sum(grad_scaled * normed, axis=(0, 1, 2))
  g_shift = jnp.sum(grad_scaled, axis=(0, 1, 2))
  late = allsum_small(jnp.stack([g_gain, g_shift]))
  token_total = lax.axis_size("dp") * samples * LAT * LON
  scale = 1.0 / math.sqrt(token_total)
  return (block_output, grad_fields) + tuple(part * scale for part in early) + (
      late[0] * scale,
      late[1] * scale,
  )


def psum_flat(parts):
    flat = jnp.concatenate([part.reshape(-1) for part in parts])
    size = flat.shape[0]
    padded = -(-size // 1024) * 1024
    flat = jnp.pad(flat, (0, padded - size)).reshape(padded // 128, 128)
    flat = lax.psum(flat, ("dp", "spatial")).reshape(-1)
    pieces, offset = [], 0
    for part in parts:
        pieces.append(flat[offset : offset + part.size].reshape(part.shape))
        offset += part.size
    return tuple(pieces)


def solution(mesh):
    return jax.shard_map(
        local,
        mesh=mesh,
        in_specs=(
            P("dp", "spatial", None, None),
            P(),
            P(),
            P(),
            P(),
            P(),
            P(),
            P("dp", "spatial", None, None),
        ),
        out_specs=(
            P("dp", "spatial", None, None),
            P("dp", "spatial", None, None),
            P(),
            P(),
            P(),
            P(),
            P(),
            P(),
        ),
        check_vma=False,
    )
```

```python
import math

import jax
import jax.numpy as jnp
from jax import lax
from jax.sharding import PartitionSpec as P


LAT = 64
LON = 128
BLOCKS = 8
BLOCK = 96


shrink_cut = 0.01
norm_epsilon = 1e-06
gelu_factor = 0.7978845608
gelu_cubic = 0.044715


def product(pattern, left_side, right_side):
    return jnp.einsum(pattern, left_side, right_side, preferred_element_type=jnp.float32)


def tables(count, mode_count, doubled):
    positions = jnp.arange(count, dtype=jnp.int32)
    orders = jnp.arange(mode_count, dtype=jnp.int32)
    phases = orders[:, None] * positions[None, :] % count
    angles = 2.0 * math.pi / count * phases.astype(jnp.float32)
    factor = jnp.ones((mode_count, 1), jnp.float32) / math.sqrt(count)
    if doubled:
        factor = factor * jnp.where(orders == 0, 1.0, 2.0).astype(jnp.float32)[:, None]
    return (
        (jnp.cos(angles) * factor).astype(jnp.bfloat16),
        (jnp.sin(angles) * factor).astype(jnp.bfloat16),
    )


def rotate(values):
    half_width = values.shape[-1] // 2
    return jnp.concatenate([values[..., half_width:], -values[..., :half_width]], axis=-1)


def along_lon(real_part, cos_table, sin_table):
    real_sum = product("bhwnp,mw->bhmnp", real_part, cos_table)
    imag_sum = -product("bhwnp,mw->bhmnp", real_part, sin_table)
    return jnp.concatenate([real_sum, imag_sum], axis=-1).astype(jnp.bfloat16)


def back_lon(spectral, cos_table, sin_table):
    half_width = spectral.shape[-1] // 2
    return product("bhmnp,mw->bhwnp", spectral[..., :half_width], cos_table) - product(
        "bhmnp,mw->bhwnp", spectral[..., half_width:], sin_table
    )


def along_lat(spectral, cos_table, sin_table):
    stacked = jnp.concatenate([spectral, rotate(spectral)], axis=1)
    table = jnp.concatenate([cos_table, sin_table], axis=1)
    return product("kh,bhmnp->bkmnp", table, stacked).astype(jnp.bfloat16)


def back_lat(spectral, cos_table, sin_table):
    stacked = jnp.concatenate([spectral, -rotate(spectral)], axis=1)
    table = jnp.concatenate([cos_table, sin_table], axis=1)
    return product("kh,bhmnp->bkmnp", table, stacked).astype(jnp.bfloat16)


def real_blocks(weight):
    upper_rows = jnp.concatenate([weight[0], weight[1]], axis=-1)
    bottom = jnp.concatenate([-weight[1], weight[0]], axis=-1)
    return jnp.concatenate([upper_rows, bottom], axis=1)


def fold_blocks(gradient):
    half_width = gradient.shape[-1] // 2
    real_grad = gradient[:, :half_width, :half_width] + gradient[:, half_width:, half_width:]
    imag_grad = gradient[:, :half_width, half_width:] - gradient[:, half_width:, :half_width]
    return jnp.stack([real_grad, imag_grad])


def gelu_value(values):
    inner = jnp.tanh(gelu_factor * (values + gelu_cubic * values * values * values))
    return 0.5 * values * (1.0 + inner)


def gelu_slope(values):
    inner = jnp.tanh(gelu_factor * (values + gelu_cubic * values * values * values))
    return 0.5 * (1.0 + inner) + 0.5 * values * (1.0 - inner * inner) * gelu_factor * (
        1.0 + 3.0 * gelu_cubic * values * values
    )


def spectral_forward(transformed, first_real, first_bias, second_real, second_bias):
    hidden_pre = product("bkmnp,npq->bkmnq", transformed, first_real) + first_bias
    hidden = gelu_value(hidden_pre).astype(jnp.bfloat16)
    output_pre = product("bkmnp,npq->bkmnq", hidden, second_real) + second_bias
    shrunk = (output_pre - shrink_cut * jnp.tanh(output_pre / shrink_cut)).astype(jnp.bfloat16)
    return (hidden_pre, hidden, output_pre, shrunk)


def spectral_backward(
    transformed, hidden_pre, hidden, output_pre, grad_shrunk, first_real, second_real
):
    bend = jnp.tanh(output_pre / shrink_cut)
    grad_outpre = (grad_shrunk.astype(jnp.float32) * bend * bend).astype(jnp.bfloat16)
    grad_second = product("bkmnp,bkmnq->npq", hidden, grad_outpre)
    grad_second_bias = jnp.sum(grad_outpre.astype(jnp.float32), axis=(0, 1, 2))
    grad_hidden = product("bkmnq,npq->bkmnp", grad_outpre, second_real)
    grad_hidpre = (grad_hidden * gelu_slope(hidden_pre)).astype(jnp.bfloat16)
    grad_first = product("bkmnp,bkmnq->npq", transformed, grad_hidpre)
    grad_first_bias = jnp.sum(grad_hidpre.astype(jnp.float32), axis=(0, 1, 2))
    grad_transformed = product("bkmnq,npq->bkmnp", grad_hidpre, first_real).astype(jnp.bfloat16)
    return (grad_transformed, grad_first, grad_first_bias, grad_second, grad_second_bias)


def normalize(fields):
    values = fields.astype(jnp.float32)
    center = jnp.mean(values, axis=-1, keepdims=True)
    spread = jnp.mean((values - center) ** 2, axis=-1, keepdims=True)
    inverse_std = lax.rsqrt(spread + norm_epsilon)
    return ((values - center) * inverse_std, inverse_std)


def norm_backward(grad_scaled, normed, inverse_std, norm_gain):
    grad_normed = grad_scaled * norm_gain
    mean_grad = jnp.mean(grad_normed, axis=-1, keepdims=True)
    mean_cross = jnp.mean(grad_normed * normed, axis=-1, keepdims=True)
    return inverse_std * (grad_normed - mean_grad - normed * mean_cross)


def send_order(me, n, size):
    chunk = (me + jnp.arange(n, dtype=jnp.int32)[:, None]) % n
    return (chunk * size + jnp.arange(size, dtype=jnp.int32)[None, :]).reshape(-1)


def receive_order(me, n, size):
    chunk = (me + n - jnp.arange(n, dtype=jnp.int32)[:, None]) % n
    return (chunk * size + jnp.arange(size, dtype=jnp.int32)[None, :]).reshape(-1)


def exchange(values, split_axis, concat_axis):
    n = lax.axis_size("spatial")
    size = values.shape[split_axis] // n
    pieces = [lax.slice_in_dim(values, k * size, (k + 1) * size, axis=split_axis) for k in range(n)]
    received = [pieces[0]] + [
        lax.ppermute(pieces[k], "spatial", [(i, (i + k) % n) for i in range(n)])
        for k in range(1, n)
    ]
    return jnp.concatenate(received, axis=concat_axis)


def allsum_small(values, axes=("spatial", "dp")):
    for axis in axes:
        n = lax.axis_size(axis)
        if n & (n - 1):
            values = lax.psum(values, axis)
            continue
        step = 1
        while step < n:
            values = values + lax.ppermute(values, axis, [(i, i ^ step) for i in range(n)])
            step *= 2
    return values


def local(
    fields, norm_gain, norm_shift, first_weight, first_bias, second_weight, second_bias, cotangent
):
  samples, band_rows, longitudes, _ = fields.shape
  mode_count = longitudes // 2
  n = lax.axis_size("spatial")
  me = lax.axis_index("spatial")
  modes_per = mode_count // n
  send_m = send_order(me, n, modes_per)
  recv_m = receive_order(me, n, modes_per)
  send_h = send_order(me, n, band_rows)
  recv_h = receive_order(me, n, band_rows)
  ahead_cos, ahead_sin = tables(longitudes, mode_count, False)
  back_cos, back_sin = tables(longitudes, mode_count, True)
  polar_cos, polar_sin = tables(LAT, LAT, False)
  first_real = real_blocks(first_weight)
  second_real = real_blocks(second_weight)
  block_shape = (samples, band_rows, longitudes, BLOCKS, BLOCK)
  normed, inverse_std = normalize(fields)
  scaled = (normed * norm_gain + norm_shift).astype(jnp.bfloat16)
  spectral = along_lon(scaled.reshape(block_shape), ahead_cos[send_m], ahead_sin[send_m])
  columns = exchange(spectral, 2, 1)
  grad_returned = along_lon(cotangent.reshape(block_shape), back_cos[send_m], back_sin[send_m])
  grad_columns = exchange(grad_returned, 2, 1)
  transformed = along_lat(columns, polar_cos[:, recv_h], polar_sin[:, recv_h])
  hidden_pre, hidden, output_pre, shrunk = spectral_forward(
      transformed, first_real, first_bias, second_real, second_bias
  )
  returned = back_lat(shrunk, polar_cos[send_h], polar_sin[send_h])
  banded = exchange(returned, 1, 2)
  grad_shrunk = along_lat(grad_columns, polar_cos[:, recv_h], polar_sin[:, recv_h])
  grad_transformed, g_first, g_first_bias, g_second, g_second_bias = spectral_backward(
      transformed, hidden_pre, hidden, output_pre, grad_shrunk, first_real, second_real
  )
  grad_spectral = back_lat(grad_transformed, polar_cos[send_h], polar_sin[send_h])
  grad_banded = exchange(grad_spectral, 1, 2)
  early = psum_flat((fold_blocks(g_first), g_first_bias, fold_blocks(g_second), g_second_bias))
  mixed = back_lon(banded, back_cos[recv_m], back_sin[recv_m]).reshape(fields.shape)
  block_output = (fields.astype(jnp.float32) + scaled.astype(jnp.float32) + mixed).astype(
      jnp.bfloat16
  )
  grad_scaled = cotangent.astype(jnp.float32) + back_lon(
      grad_banded, ahead_cos[recv_m], ahead_sin[recv_m]
  ).reshape(fields.shape)
  grad_fields = (
      cotangent.astype(jnp.float32) + norm_backward(grad_scaled, normed, inverse_std, norm_gain)
  ).astype(jnp.bfloat16)
  g_gain = jnp.sum(grad_scaled * normed, axis=(0, 1, 2))
  g_shift = jnp.sum(grad_scaled, axis=(0, 1, 2))
  late = allsum_small(jnp.stack([g_gain, g_shift]))
  token_total = lax.axis_size("dp") * samples * LAT * LON
  scale = 1.0 / math.sqrt(token_total)
  return (block_output, grad_fields) + tuple(part * scale for part in early) + (
      late[0] * scale,
      late[1] * scale,
  )


def psum_flat(parts):
    flat = jnp.concatenate([part.reshape(-1) for part in parts])
    size = flat.shape[0]
    unit = 1024 * lax.axis_size("dp")
    padded = -(-size // unit) * unit
    flat = jnp.pad(flat, (0, padded - size)).reshape(padded // 128, 128)
    flat = allsum_large(flat).reshape(-1)
    pieces, offset = [], 0
    for part in parts:
        pieces.append(flat[offset : offset + part.size].reshape(part.shape))
        offset += part.size
    return tuple(pieces)


def allsum_large(values):
    n = lax.axis_size("dp")
    if n & (n - 1):
        return lax.psum(values, ("dp", "spatial"))
    me = lax.axis_index("dp")
    bits = []
    step = 1
    while step < n:
        bits.append(step)
        step *= 2
    for step in bits:
        half = values.shape[0] // 2
        high = (me // step) % 2
        keep = lax.dynamic_slice_in_dim(values, high * half, half, axis=0)
        send = lax.dynamic_slice_in_dim(values, (1 - high) * half, half, axis=0)
        values = keep + lax.ppermute(send, "dp", [(i, i ^ step) for i in range(n)])
    values = allsum_small(values, ("spatial",))
    for step in reversed(bits):
        high = (me // step) % 2
        other = lax.ppermute(values, "dp", [(i, i ^ step) for i in range(n)])
        values = jnp.where(
            high == 0,
            jnp.concatenate([values, other], axis=0),
            jnp.concatenate([other, values], axis=0),
        )
    return values


def solution(mesh):
    return jax.shard_map(
        local,
        mesh=mesh,
        in_specs=(
            P("dp", "spatial", None, None),
            P(),
            P(),
            P(),
            P(),
            P(),
            P(),
            P("dp", "spatial", None, None),
        ),
        out_specs=(
            P("dp", "spatial", None, None),
            P("dp", "spatial", None, None),
            P(),
            P(),
            P(),
            P(),
            P(),
            P(),
        ),
        check_vma=False,
    )
```

```python
import math

import jax
import jax.numpy as jnp
from jax import lax
from jax.sharding import PartitionSpec as P


LAT = 64
LON = 128
BLOCKS = 8
BLOCK = 96


shrink_cut = 0.01
norm_epsilon = 1e-06
gelu_factor = 0.7978845608
gelu_cubic = 0.044715


def product(pattern, left_side, right_side):
    return jnp.einsum(pattern, left_side, right_side, preferred_element_type=jnp.float32)


def tables(count, mode_count, doubled):
    positions = jnp.arange(count, dtype=jnp.int32)
    orders = jnp.arange(mode_count, dtype=jnp.int32)
    phases = orders[:, None] * positions[None, :] % count
    angles = 2.0 * math.pi / count * phases.astype(jnp.float32)
    factor = jnp.ones((mode_count, 1), jnp.float32) / math.sqrt(count)
    if doubled:
        factor = factor * jnp.where(orders == 0, 1.0, 2.0).astype(jnp.float32)[:, None]
    return (
        (jnp.cos(angles) * factor).astype(jnp.bfloat16),
        (jnp.sin(angles) * factor).astype(jnp.bfloat16),
    )


def rotate(values):
    half_width = values.shape[-1] // 2
    return jnp.concatenate([values[..., half_width:], -values[..., :half_width]], axis=-1)


def along_lon(real_part, cos_table, sin_table):
    real_sum = product("bhwnp,mw->bhmnp", real_part, cos_table)
    imag_sum = -product("bhwnp,mw->bhmnp", real_part, sin_table)
    return jnp.concatenate([real_sum, imag_sum], axis=-1).astype(jnp.bfloat16)


def back_lon(spectral, cos_table, sin_table):
    half_width = spectral.shape[-1] // 2
    return product("bhmnp,mw->bhwnp", spectral[..., :half_width], cos_table) - product(
        "bhmnp,mw->bhwnp", spectral[..., half_width:], sin_table
    )


def along_lat(spectral, cos_table, sin_table):
    stacked = jnp.concatenate([spectral, rotate(spectral)], axis=1)
    table = jnp.concatenate([cos_table, sin_table], axis=1)
    return product("kh,bhmnp->bkmnp", table, stacked).astype(jnp.bfloat16)


def back_lat(spectral, cos_table, sin_table):
    stacked = jnp.concatenate([spectral, -rotate(spectral)], axis=1)
    table = jnp.concatenate([cos_table, sin_table], axis=1)
    return product("kh,bhmnp->bkmnp", table, stacked).astype(jnp.bfloat16)


def real_blocks(weight):
    upper_rows = jnp.concatenate([weight[0], weight[1]], axis=-1)
    bottom = jnp.concatenate([-weight[1], weight[0]], axis=-1)
    return jnp.concatenate([upper_rows, bottom], axis=1)


def fold_blocks(gradient):
    half_width = gradient.shape[-1] // 2
    real_grad = gradient[:, :half_width, :half_width] + gradient[:, half_width:, half_width:]
    imag_grad = gradient[:, :half_width, half_width:] - gradient[:, half_width:, :half_width]
    return jnp.stack([real_grad, imag_grad])


def gelu_value(values):
    inner = jnp.tanh(gelu_factor * (values + gelu_cubic * values * values * values))
    return 0.5 * values * (1.0 + inner)


def gelu_slope(values):
    inner = jnp.tanh(gelu_factor * (values + gelu_cubic * values * values * values))
    return 0.5 * (1.0 + inner) + 0.5 * values * (1.0 - inner * inner) * gelu_factor * (
        1.0 + 3.0 * gelu_cubic * values * values
    )


def spectral_forward(transformed, first_real, first_bias, second_real, second_bias):
    hidden_pre = product("bkmnp,npq->bkmnq", transformed, first_real) + first_bias
    hidden = gelu_value(hidden_pre).astype(jnp.bfloat16)
    output_pre = product("bkmnp,npq->bkmnq", hidden, second_real) + second_bias
    shrunk = (output_pre - shrink_cut * jnp.tanh(output_pre / shrink_cut)).astype(jnp.bfloat16)
    return (hidden_pre, hidden, output_pre, shrunk)


def spectral_backward(
    transformed, hidden_pre, hidden, output_pre, grad_shrunk, first_real, second_real
):
    bend = jnp.tanh(output_pre / shrink_cut)
    grad_outpre = (grad_shrunk.astype(jnp.float32) * bend * bend).astype(jnp.bfloat16)
    grad_second = product("bkmnp,bkmnq->npq", hidden, grad_outpre)
    grad_second_bias = jnp.sum(grad_outpre.astype(jnp.float32), axis=(0, 1, 2))
    grad_hidden = product("bkmnq,npq->bkmnp", grad_outpre, second_real)
    grad_hidpre = (grad_hidden * gelu_slope(hidden_pre)).astype(jnp.bfloat16)
    grad_first = product("bkmnp,bkmnq->npq", transformed, grad_hidpre)
    grad_first_bias = jnp.sum(grad_hidpre.astype(jnp.float32), axis=(0, 1, 2))
    grad_transformed = product("bkmnq,npq->bkmnp", grad_hidpre, first_real).astype(jnp.bfloat16)
    return (grad_transformed, grad_first, grad_first_bias, grad_second, grad_second_bias)


def normalize(fields):
    values = fields.astype(jnp.float32)
    center = jnp.mean(values, axis=-1, keepdims=True)
    spread = jnp.mean((values - center) ** 2, axis=-1, keepdims=True)
    inverse_std = lax.rsqrt(spread + norm_epsilon)
    return ((values - center) * inverse_std, inverse_std)


def norm_backward(grad_scaled, normed, inverse_std, norm_gain):
    grad_normed = grad_scaled * norm_gain
    mean_grad = jnp.mean(grad_normed, axis=-1, keepdims=True)
    mean_cross = jnp.mean(grad_normed * normed, axis=-1, keepdims=True)
    return inverse_std * (grad_normed - mean_grad - normed * mean_cross)


def send_order(me, n, size):
    chunk = (me + jnp.arange(n, dtype=jnp.int32)[:, None]) % n
    return (chunk * size + jnp.arange(size, dtype=jnp.int32)[None, :]).reshape(-1)


def receive_order(me, n, size):
    chunk = (me + n - jnp.arange(n, dtype=jnp.int32)[:, None]) % n
    return (chunk * size + jnp.arange(size, dtype=jnp.int32)[None, :]).reshape(-1)


def exchange(values, split_axis, concat_axis):
    n = lax.axis_size("spatial")
    size = values.shape[split_axis] // n
    pieces = [lax.slice_in_dim(values, k * size, (k + 1) * size, axis=split_axis) for k in range(n)]
    received = [pieces[0]] + [
        lax.ppermute(pieces[k], "spatial", [(i, (i + k) % n) for i in range(n)])
        for k in range(1, n)
    ]
    return jnp.concatenate(received, axis=concat_axis)


def allsum_small(values, axes=("spatial", "dp")):
    for axis in axes:
        n = lax.axis_size(axis)
        if n & (n - 1):
            values = lax.psum(values, axis)
            continue
        step = 1
        while step < n:
            values = values + lax.ppermute(values, axis, [(i, i ^ step) for i in range(n)])
            step *= 2
    return values


def local(
    fields, norm_gain, norm_shift, first_weight, first_bias, second_weight, second_bias, cotangent
):
  samples, band_rows, longitudes, _ = fields.shape
  mode_count = longitudes // 2
  n = lax.axis_size("spatial")
  me = lax.axis_index("spatial")
  modes_per = mode_count // n
  send_m = send_order(me, n, modes_per)
  recv_m = receive_order(me, n, modes_per)
  send_h = send_order(me, n, band_rows)
  recv_h = receive_order(me, n, band_rows)
  ahead_cos, ahead_sin = tables(longitudes, mode_count, False)
  back_cos, back_sin = tables(longitudes, mode_count, True)
  polar_cos, polar_sin = tables(LAT, LAT, False)
  first_real = real_blocks(first_weight)
  second_real = real_blocks(second_weight)
  block_shape = (samples, band_rows, longitudes, BLOCKS, BLOCK)
  normed, inverse_std = normalize(fields)
  scaled = (normed * norm_gain + norm_shift).astype(jnp.bfloat16)
  spectral = along_lon(scaled.reshape(block_shape), ahead_cos[send_m], ahead_sin[send_m])
  columns = exchange(spectral, 2, 1)
  grad_returned = along_lon(cotangent.reshape(block_shape), back_cos[send_m], back_sin[send_m])
  grad_columns = exchange(grad_returned, 2, 1)
  transformed = along_lat(columns, polar_cos[:, recv_h], polar_sin[:, recv_h])
  hidden_pre, hidden, output_pre, shrunk = spectral_forward(
      transformed, first_real, first_bias, second_real, second_bias
  )
  returned = back_lat(shrunk, polar_cos[send_h], polar_sin[send_h])
  banded = exchange(returned, 1, 2)
  halves = []
  for lo, hi in ((0, BLOCKS // 2), (BLOCKS // 2, BLOCKS)):
      pick = lambda values: values[:, :, :, lo:hi]
      grad_shrunk = along_lat(pick(grad_columns), polar_cos[:, recv_h], polar_sin[:, recv_h])
      grad_transformed, g_first, g_first_bias, g_second, g_second_bias = spectral_backward(
          pick(transformed),
          pick(hidden_pre),
          pick(hidden),
          pick(output_pre),
          grad_shrunk,
          first_real[lo:hi],
          second_real[lo:hi],
      )
      grad_spectral = back_lat(grad_transformed, polar_cos[send_h], polar_sin[send_h])
      grad_banded = exchange(grad_spectral, 1, 2)
      halves.append((grad_banded, g_first, g_first_bias, g_second, g_second_bias))
  grad_banded, g_first, g_first_bias, g_second, g_second_bias = (
      jnp.concatenate(parts, axis=axis) for parts, axis in zip(zip(*halves), (3, 0, 0, 0, 0))
  )
  early = psum_flat((fold_blocks(g_first), g_first_bias, fold_blocks(g_second), g_second_bias))
  mixed = back_lon(banded, back_cos[recv_m], back_sin[recv_m]).reshape(fields.shape)
  block_output = (fields.astype(jnp.float32) + scaled.astype(jnp.float32) + mixed).astype(
      jnp.bfloat16
  )
  grad_scaled = cotangent.astype(jnp.float32) + back_lon(
      grad_banded, ahead_cos[recv_m], ahead_sin[recv_m]
  ).reshape(fields.shape)
  grad_fields = (
      cotangent.astype(jnp.float32) + norm_backward(grad_scaled, normed, inverse_std, norm_gain)
  ).astype(jnp.bfloat16)
  g_gain = jnp.sum(grad_scaled * normed, axis=(0, 1, 2))
  g_shift = jnp.sum(grad_scaled, axis=(0, 1, 2))
  late = allsum_small(jnp.stack([g_gain, g_shift]))
  token_total = lax.axis_size("dp") * samples * LAT * LON
  scale = 1.0 / math.sqrt(token_total)
  return (block_output, grad_fields) + tuple(part * scale for part in early) + (
      late[0] * scale,
      late[1] * scale,
  )


def psum_flat(parts):
    flat = jnp.concatenate([part.reshape(-1) for part in parts])
    size = flat.shape[0]
    unit = 1024 * lax.axis_size("dp")
    padded = -(-size // unit) * unit
    flat = jnp.pad(flat, (0, padded - size)).reshape(padded // 128, 128)
    flat = allsum_large(flat).reshape(-1)
    pieces, offset = [], 0
    for part in parts:
        pieces.append(flat[offset : offset + part.size].reshape(part.shape))
        offset += part.size
    return tuple(pieces)


def allsum_large(values):
    n = lax.axis_size("dp")
    if n & (n - 1):
        return lax.psum(values, ("dp", "spatial"))
    me = lax.axis_index("dp")
    bits = []
    step = 1
    while step < n:
        bits.append(step)
        step *= 2
    for step in bits:
        half = values.shape[0] // 2
        high = (me // step) % 2
        keep = lax.dynamic_slice_in_dim(values, high * half, half, axis=0)
        send = lax.dynamic_slice_in_dim(values, (1 - high) * half, half, axis=0)
        values = keep + lax.ppermute(send, "dp", [(i, i ^ step) for i in range(n)])
    values = allsum_small(values, ("spatial",))
    for step in reversed(bits):
        high = (me // step) % 2
        other = lax.ppermute(values, "dp", [(i, i ^ step) for i in range(n)])
        values = jnp.where(
            high == 0,
            jnp.concatenate([values, other], axis=0),
            jnp.concatenate([other, values], axis=0),
        )
    return values


def solution(mesh):
    return jax.shard_map(
        local,
        mesh=mesh,
        in_specs=(
            P("dp", "spatial", None, None),
            P(),
            P(),
            P(),
            P(),
            P(),
            P(),
            P("dp", "spatial", None, None),
        ),
        out_specs=(
            P("dp", "spatial", None, None),
            P("dp", "spatial", None, None),
            P(),
            P(),
            P(),
            P(),
            P(),
            P(),
        ),
        check_vma=False,
    )
```

```python
import math

import jax
import jax.numpy as jnp
from jax import lax
from jax.sharding import PartitionSpec as P


LAT = 64
LON = 128
BLOCKS = 8
BLOCK = 96


shrink_cut = 0.01
norm_epsilon = 1e-06
gelu_factor = 0.7978845608
gelu_cubic = 0.044715


def product(pattern, left_side, right_side):
    return jnp.einsum(pattern, left_side, right_side, preferred_element_type=jnp.float32)


def tables(count, mode_count, doubled):
    positions = jnp.arange(count, dtype=jnp.int32)
    orders = jnp.arange(mode_count, dtype=jnp.int32)
    phases = orders[:, None] * positions[None, :] % count
    angles = 2.0 * math.pi / count * phases.astype(jnp.float32)
    factor = jnp.ones((mode_count, 1), jnp.float32) / math.sqrt(count)
    if doubled:
        factor = factor * jnp.where(orders == 0, 1.0, 2.0).astype(jnp.float32)[:, None]
    return (
        (jnp.cos(angles) * factor).astype(jnp.bfloat16),
        (jnp.sin(angles) * factor).astype(jnp.bfloat16),
    )


def rotate(values):
    half_width = values.shape[-1] // 2
    return jnp.concatenate([values[..., half_width:], -values[..., :half_width]], axis=-1)


def along_lon(real_part, cos_table, sin_table):
    real_sum = product("bhwnp,mw->bhmnp", real_part, cos_table)
    imag_sum = -product("bhwnp,mw->bhmnp", real_part, sin_table)
    return jnp.concatenate([real_sum, imag_sum], axis=-1).astype(jnp.bfloat16)


def back_lon(spectral, cos_table, sin_table):
    half_width = spectral.shape[-1] // 2
    return product("bhmnp,mw->bhwnp", spectral[..., :half_width], cos_table) - product(
        "bhmnp,mw->bhwnp", spectral[..., half_width:], sin_table
    )


def along_lat(spectral, cos_table, sin_table):
    stacked = jnp.concatenate([spectral, rotate(spectral)], axis=1)
    table = jnp.concatenate([cos_table, sin_table], axis=1)
    return product("kh,bhmnp->bkmnp", table, stacked).astype(jnp.bfloat16)


def back_lat(spectral, cos_table, sin_table):
    stacked = jnp.concatenate([spectral, -rotate(spectral)], axis=1)
    table = jnp.concatenate([cos_table, sin_table], axis=1)
    return product("kh,bhmnp->bkmnp", table, stacked).astype(jnp.bfloat16)


def real_blocks(weight):
    upper_rows = jnp.concatenate([weight[0], weight[1]], axis=-1)
    bottom = jnp.concatenate([-weight[1], weight[0]], axis=-1)
    return jnp.concatenate([upper_rows, bottom], axis=1)


def fold_blocks(gradient):
    half_width = gradient.shape[-1] // 2
    real_grad = gradient[:, :half_width, :half_width] + gradient[:, half_width:, half_width:]
    imag_grad = gradient[:, :half_width, half_width:] - gradient[:, half_width:, :half_width]
    return jnp.stack([real_grad, imag_grad])


def gelu_value(values):
    inner = jnp.tanh(gelu_factor * (values + gelu_cubic * values * values * values))
    return 0.5 * values * (1.0 + inner)


def gelu_slope(values):
    inner = jnp.tanh(gelu_factor * (values + gelu_cubic * values * values * values))
    return 0.5 * (1.0 + inner) + 0.5 * values * (1.0 - inner * inner) * gelu_factor * (
        1.0 + 3.0 * gelu_cubic * values * values
    )


def spectral_forward(transformed, first_real, first_bias, second_real, second_bias):
    hidden_pre = product("bkmnp,npq->bkmnq", transformed, first_real) + first_bias
    hidden = gelu_value(hidden_pre).astype(jnp.bfloat16)
    output_pre = product("bkmnp,npq->bkmnq", hidden, second_real) + second_bias
    shrunk = (output_pre - shrink_cut * jnp.tanh(output_pre / shrink_cut)).astype(jnp.bfloat16)
    return (hidden_pre, hidden, output_pre, shrunk)


def spectral_backward(
    transformed, hidden_pre, hidden, output_pre, grad_shrunk, first_real, second_real
):
    bend = jnp.tanh(output_pre / shrink_cut)
    grad_outpre = (grad_shrunk.astype(jnp.float32) * bend * bend).astype(jnp.bfloat16)
    grad_second = product("bkmnp,bkmnq->npq", hidden, grad_outpre)
    grad_second_bias = jnp.sum(grad_outpre.astype(jnp.float32), axis=(0, 1, 2))
    grad_hidden = product("bkmnq,npq->bkmnp", grad_outpre, second_real)
    grad_hidpre = (grad_hidden * gelu_slope(hidden_pre)).astype(jnp.bfloat16)
    grad_first = product("bkmnp,bkmnq->npq", transformed, grad_hidpre)
    grad_first_bias = jnp.sum(grad_hidpre.astype(jnp.float32), axis=(0, 1, 2))
    grad_transformed = product("bkmnq,npq->bkmnp", grad_hidpre, first_real).astype(jnp.bfloat16)
    return (grad_transformed, grad_first, grad_first_bias, grad_second, grad_second_bias)


def normalize(fields):
    values = fields.astype(jnp.float32)
    center = jnp.mean(values, axis=-1, keepdims=True)
    spread = jnp.mean((values - center) ** 2, axis=-1, keepdims=True)
    inverse_std = lax.rsqrt(spread + norm_epsilon)
    return ((values - center) * inverse_std, inverse_std)


def norm_backward(grad_scaled, normed, inverse_std, norm_gain):
    grad_normed = grad_scaled * norm_gain
    mean_grad = jnp.mean(grad_normed, axis=-1, keepdims=True)
    mean_cross = jnp.mean(grad_normed * normed, axis=-1, keepdims=True)
    return inverse_std * (grad_normed - mean_grad - normed * mean_cross)


def send_order(me, n, size):
    chunk = (me + jnp.arange(n, dtype=jnp.int32)[:, None]) % n
    return (chunk * size + jnp.arange(size, dtype=jnp.int32)[None, :]).reshape(-1)


def receive_order(me, n, size):
    chunk = (me + n - jnp.arange(n, dtype=jnp.int32)[:, None]) % n
    return (chunk * size + jnp.arange(size, dtype=jnp.int32)[None, :]).reshape(-1)


def exchange(values, split_axis, concat_axis):
    n = lax.axis_size("spatial")
    size = values.shape[split_axis] // n
    pieces = [lax.slice_in_dim(values, k * size, (k + 1) * size, axis=split_axis) for k in range(n)]
    received = [pieces[0]] + [
        lax.ppermute(pieces[k], "spatial", [(i, (i + k) % n) for i in range(n)])
        for k in range(1, n)
    ]
    return jnp.concatenate(received, axis=concat_axis)


def shifted(values, axis, n):
    return [values] + [
        lax.ppermute(values, axis, [(i, (i + k) % n) for i in range(n)]) for k in range(1, n)
    ]


def by_source(received, me, n):
    stacked = jnp.stack(received)
    return jnp.take(stacked, (me + n - jnp.arange(n, dtype=jnp.int32)) % n, axis=0)


def allsum_round(values, axis):
    n = lax.axis_size(axis)
    me = lax.axis_index(axis)
    return jnp.sum(by_source(shifted(values, axis, n), me, n), axis=0)


def allsum_small(values):
    return allsum_round(allsum_round(values, "spatial"), "dp")


def local(
    fields, norm_gain, norm_shift, first_weight, first_bias, second_weight, second_bias, cotangent
):
  samples, band_rows, longitudes, _ = fields.shape
  mode_count = longitudes // 2
  n = lax.axis_size("spatial")
  me = lax.axis_index("spatial")
  modes_per = mode_count // n
  send_m = send_order(me, n, modes_per)
  recv_m = receive_order(me, n, modes_per)
  send_h = send_order(me, n, band_rows)
  recv_h = receive_order(me, n, band_rows)
  ahead_cos, ahead_sin = tables(longitudes, mode_count, False)
  back_cos, back_sin = tables(longitudes, mode_count, True)
  polar_cos, polar_sin = tables(LAT, LAT, False)
  first_real = real_blocks(first_weight)
  second_real = real_blocks(second_weight)
  block_shape = (samples, band_rows, longitudes, BLOCKS, BLOCK)
  normed, inverse_std = normalize(fields)
  scaled = (normed * norm_gain + norm_shift).astype(jnp.bfloat16)
  spectral = along_lon(scaled.reshape(block_shape), ahead_cos[send_m], ahead_sin[send_m])
  columns = exchange(spectral, 2, 1)
  grad_returned = along_lon(cotangent.reshape(block_shape), back_cos[send_m], back_sin[send_m])
  grad_columns = exchange(grad_returned, 2, 1)
  transformed = along_lat(columns, polar_cos[:, recv_h], polar_sin[:, recv_h])
  hidden_pre, hidden, output_pre, shrunk = spectral_forward(
      transformed, first_real, first_bias, second_real, second_bias
  )
  returned = back_lat(shrunk, polar_cos[send_h], polar_sin[send_h])
  banded = exchange(returned, 1, 2)
  halves = []
  for lo, hi in ((0, BLOCKS // 2), (BLOCKS // 2, BLOCKS)):
      pick = lambda values: values[:, :, :, lo:hi]
      grad_shrunk = along_lat(pick(grad_columns), polar_cos[:, recv_h], polar_sin[:, recv_h])
      grad_transformed, g_first, g_first_bias, g_second, g_second_bias = spectral_backward(
          pick(transformed),
          pick(hidden_pre),
          pick(hidden),
          pick(output_pre),
          grad_shrunk,
          first_real[lo:hi],
          second_real[lo:hi],
      )
      grad_spectral = back_lat(grad_transformed, polar_cos[send_h], polar_sin[send_h])
      grad_banded = exchange(grad_spectral, 1, 2)
      halves.append((grad_banded, g_first, g_first_bias, g_second, g_second_bias))
  grad_banded, g_first, g_first_bias, g_second, g_second_bias = (
      jnp.concatenate(parts, axis=axis) for parts, axis in zip(zip(*halves), (3, 0, 0, 0, 0))
  )
  early = psum_flat((fold_blocks(g_first), g_first_bias, fold_blocks(g_second), g_second_bias))
  mixed = back_lon(banded, back_cos[recv_m], back_sin[recv_m]).reshape(fields.shape)
  block_output = (fields.astype(jnp.float32) + scaled.astype(jnp.float32) + mixed).astype(
      jnp.bfloat16
  )
  grad_scaled = cotangent.astype(jnp.float32) + back_lon(
      grad_banded, ahead_cos[recv_m], ahead_sin[recv_m]
  ).reshape(fields.shape)
  grad_fields = (
      cotangent.astype(jnp.float32) + norm_backward(grad_scaled, normed, inverse_std, norm_gain)
  ).astype(jnp.bfloat16)
  g_gain = jnp.sum(grad_scaled * normed, axis=(0, 1, 2))
  g_shift = jnp.sum(grad_scaled, axis=(0, 1, 2))
  late = allsum_small(jnp.stack([g_gain, g_shift]))
  token_total = lax.axis_size("dp") * samples * LAT * LON
  scale = 1.0 / math.sqrt(token_total)
  return (block_output, grad_fields) + tuple(part * scale for part in early) + (
      late[0] * scale,
      late[1] * scale,
  )


def psum_flat(parts):
    flat = jnp.concatenate([part.reshape(-1) for part in parts])
    size = flat.shape[0]
    unit = 1024 * lax.axis_size("dp")
    padded = -(-size // unit) * unit
    flat = jnp.pad(flat, (0, padded - size)).reshape(padded // 128, 128)
    flat = allsum_large(flat).reshape(-1)
    pieces, offset = [], 0
    for part in parts:
        pieces.append(flat[offset : offset + part.size].reshape(part.shape))
        offset += part.size
    return tuple(pieces)


def allsum_large(values):
    n = lax.axis_size("dp")
    me = lax.axis_index("dp")
    chunks = values.reshape((n, values.shape[0] // n) + values.shape[1:])
    parts = [chunks[me]] + [
        lax.ppermute(chunks[(me + k) % n], "dp", [(i, (i + k) % n) for i in range(n)])
        for k in range(1, n)
    ]
    owned = allsum_round(jnp.sum(jnp.stack(parts), axis=0), "spatial")
    return by_source(shifted(owned, "dp", n), me, n).reshape(values.shape)


def solution(mesh):
    return jax.shard_map(
        local,
        mesh=mesh,
        in_specs=(
            P("dp", "spatial", None, None),
            P(),
            P(),
            P(),
            P(),
            P(),
            P(),
            P("dp", "spatial", None, None),
        ),
        out_specs=(
            P("dp", "spatial", None, None),
            P("dp", "spatial", None, None),
            P(),
            P(),
            P(),
            P(),
            P(),
            P(),
        ),
        check_vma=False,
    )
```

```python
import math

import jax
import jax.numpy as jnp
from jax import lax
from jax.sharding import PartitionSpec as P


LAT = 64
LON = 128
BLOCKS = 8
BLOCK = 96


shrink_cut = 0.01
norm_epsilon = 1e-06
gelu_factor = 0.7978845608
gelu_cubic = 0.044715


def product(pattern, left_side, right_side):
    return jnp.einsum(pattern, left_side, right_side, preferred_element_type=jnp.float32)


def tables(count, mode_count, doubled):
    positions = jnp.arange(count, dtype=jnp.int32)
    orders = jnp.arange(mode_count, dtype=jnp.int32)
    phases = orders[:, None] * positions[None, :] % count
    angles = 2.0 * math.pi / count * phases.astype(jnp.float32)
    factor = jnp.ones((mode_count, 1), jnp.float32) / math.sqrt(count)
    if doubled:
        factor = factor * jnp.where(orders == 0, 1.0, 2.0).astype(jnp.float32)[:, None]
    return (
        (jnp.cos(angles) * factor).astype(jnp.bfloat16),
        (jnp.sin(angles) * factor).astype(jnp.bfloat16),
    )


def rotate(values):
    half_width = values.shape[-1] // 2
    return jnp.concatenate([values[..., half_width:], -values[..., :half_width]], axis=-1)


def along_lon(real_part, cos_table, sin_table):
    real_sum = product("bhwnp,mw->bhmnp", real_part, cos_table)
    imag_sum = -product("bhwnp,mw->bhmnp", real_part, sin_table)
    return jnp.concatenate([real_sum, imag_sum], axis=-1).astype(jnp.bfloat16)


def back_lon(spectral, cos_table, sin_table):
    half_width = spectral.shape[-1] // 2
    return product("bhmnp,mw->bhwnp", spectral[..., :half_width], cos_table) - product(
        "bhmnp,mw->bhwnp", spectral[..., half_width:], sin_table
    )


def along_lat(spectral, cos_table, sin_table):
    stacked = jnp.concatenate([spectral, rotate(spectral)], axis=1)
    table = jnp.concatenate([cos_table, sin_table], axis=1)
    return product("kh,bhmnp->bkmnp", table, stacked).astype(jnp.bfloat16)


def back_lat(spectral, cos_table, sin_table):
    stacked = jnp.concatenate([spectral, -rotate(spectral)], axis=1)
    table = jnp.concatenate([cos_table, sin_table], axis=1)
    return product("kh,bhmnp->bkmnp", table, stacked).astype(jnp.bfloat16)


def real_blocks(weight):
    upper_rows = jnp.concatenate([weight[0], weight[1]], axis=-1)
    bottom = jnp.concatenate([-weight[1], weight[0]], axis=-1)
    return jnp.concatenate([upper_rows, bottom], axis=1)


def fold_blocks(gradient):
    half_width = gradient.shape[-1] // 2
    real_grad = gradient[:, :half_width, :half_width] + gradient[:, half_width:, half_width:]
    imag_grad = gradient[:, :half_width, half_width:] - gradient[:, half_width:, :half_width]
    return jnp.stack([real_grad, imag_grad])


def gelu_value(values):
    inner = jnp.tanh(gelu_factor * (values + gelu_cubic * values * values * values))
    return 0.5 * values * (1.0 + inner)


def gelu_slope(values):
    inner = jnp.tanh(gelu_factor * (values + gelu_cubic * values * values * values))
    return 0.5 * (1.0 + inner) + 0.5 * values * (1.0 - inner * inner) * gelu_factor * (
        1.0 + 3.0 * gelu_cubic * values * values
    )


def spectral_forward(transformed, first_real, first_bias, second_real, second_bias):
    hidden_pre = product("bkmnp,npq->bkmnq", transformed, first_real) + first_bias
    hidden = gelu_value(hidden_pre).astype(jnp.bfloat16)
    output_pre = product("bkmnp,npq->bkmnq", hidden, second_real) + second_bias
    shrunk = (output_pre - shrink_cut * jnp.tanh(output_pre / shrink_cut)).astype(jnp.bfloat16)
    return (hidden_pre, hidden, output_pre, shrunk)


def spectral_backward(
    transformed, hidden_pre, hidden, output_pre, grad_shrunk, first_real, second_real
):
    bend = jnp.tanh(output_pre / shrink_cut)
    grad_outpre = (grad_shrunk.astype(jnp.float32) * bend * bend).astype(jnp.bfloat16)
    grad_second = product("bkmnp,bkmnq->npq", hidden, grad_outpre)
    grad_second_bias = jnp.sum(grad_outpre.astype(jnp.float32), axis=(0, 1, 2))
    grad_hidden = product("bkmnq,npq->bkmnp", grad_outpre, second_real)
    grad_hidpre = (grad_hidden * gelu_slope(hidden_pre)).astype(jnp.bfloat16)
    grad_first = product("bkmnp,bkmnq->npq", transformed, grad_hidpre)
    grad_first_bias = jnp.sum(grad_hidpre.astype(jnp.float32), axis=(0, 1, 2))
    grad_transformed = product("bkmnq,npq->bkmnp", grad_hidpre, first_real).astype(jnp.bfloat16)
    return (grad_transformed, grad_first, grad_first_bias, grad_second, grad_second_bias)


def normalize(fields):
    values = fields.astype(jnp.float32)
    center = jnp.mean(values, axis=-1, keepdims=True)
    spread = jnp.mean((values - center) ** 2, axis=-1, keepdims=True)
    inverse_std = lax.rsqrt(spread + norm_epsilon)
    return ((values - center) * inverse_std, inverse_std)


def norm_backward(grad_scaled, normed, inverse_std, norm_gain):
    grad_normed = grad_scaled * norm_gain
    mean_grad = jnp.mean(grad_normed, axis=-1, keepdims=True)
    mean_cross = jnp.mean(grad_normed * normed, axis=-1, keepdims=True)
    return inverse_std * (grad_normed - mean_grad - normed * mean_cross)


def send_order(me, n, size):
    chunk = (me + jnp.arange(n, dtype=jnp.int32)[:, None]) % n
    return (chunk * size + jnp.arange(size, dtype=jnp.int32)[None, :]).reshape(-1)


def receive_order(me, n, size):
    chunk = (me + n - jnp.arange(n, dtype=jnp.int32)[:, None]) % n
    return (chunk * size + jnp.arange(size, dtype=jnp.int32)[None, :]).reshape(-1)


def exchange(values, split_axis, concat_axis):
    n = lax.axis_size("spatial")
    size = values.shape[split_axis] // n
    pieces = [lax.slice_in_dim(values, k * size, (k + 1) * size, axis=split_axis) for k in range(n)]
    received = [pieces[0]] + [
        lax.ppermute(pieces[k], "spatial", [(i, (i + k) % n) for i in range(n)])
        for k in range(1, n)
    ]
    return jnp.concatenate(received, axis=concat_axis)


def allsum_small(values, axes=("spatial", "dp")):
    for axis in axes:
        n = lax.axis_size(axis)
        if n & (n - 1):
            values = lax.psum(values, axis)
            continue
        step = 1
        while step < n:
            values = values + lax.ppermute(values, axis, [(i, i ^ step) for i in range(n)])
            step *= 2
    return values


def local(
    fields, norm_gain, norm_shift, first_weight, first_bias, second_weight, second_bias, cotangent
):
  samples, band_rows, longitudes, _ = fields.shape
  mode_count = longitudes // 2
  n = lax.axis_size("spatial")
  me = lax.axis_index("spatial")
  modes_per = mode_count // n
  send_m = send_order(me, n, modes_per)
  recv_m = receive_order(me, n, modes_per)
  send_h = send_order(me, n, band_rows)
  recv_h = receive_order(me, n, band_rows)
  ahead_cos, ahead_sin = tables(longitudes, mode_count, False)
  back_cos, back_sin = tables(longitudes, mode_count, True)
  polar_cos, polar_sin = tables(LAT, LAT, False)
  first_real = real_blocks(first_weight)
  second_real = real_blocks(second_weight)
  block_shape = (samples, band_rows, longitudes, BLOCKS, BLOCK)
  normed, inverse_std = normalize(fields)
  scaled = (normed * norm_gain + norm_shift).astype(jnp.bfloat16)
  spectral = along_lon(scaled.reshape(block_shape), ahead_cos[send_m], ahead_sin[send_m])
  columns = exchange(spectral, 2, 1)
  grad_returned = along_lon(cotangent.reshape(block_shape), back_cos[send_m], back_sin[send_m])
  grad_columns = exchange(grad_returned, 2, 1)
  transformed = along_lat(columns, polar_cos[:, recv_h], polar_sin[:, recv_h])
  hidden_pre, hidden, output_pre, shrunk = spectral_forward(
      transformed, first_real, first_bias, second_real, second_bias
  )
  returned = back_lat(shrunk, polar_cos[send_h], polar_sin[send_h])
  banded = exchange(returned, 1, 2)
  halves = []
  for lo, hi in ((0, BLOCKS // 2), (BLOCKS // 2, BLOCKS)):
      pick = lambda values: values[:, :, :, lo:hi]
      grad_shrunk = along_lat(pick(grad_columns), polar_cos[:, recv_h], polar_sin[:, recv_h])
      grad_transformed, g_first, g_first_bias, g_second, g_second_bias = spectral_backward(
          pick(transformed),
          pick(hidden_pre),
          pick(hidden),
          pick(output_pre),
          grad_shrunk,
          first_real[lo:hi],
          second_real[lo:hi],
      )
      grad_spectral = back_lat(grad_transformed, polar_cos[send_h], polar_sin[send_h])
      grad_banded = exchange(grad_spectral, 1, 2)
      summed = psum_flat((fold_blocks(g_first), g_first_bias, fold_blocks(g_second), g_second_bias))
      halves.append((grad_banded,) + summed)
  grad_banded, g_first, g_first_bias, g_second, g_second_bias = (
      jnp.concatenate(parts, axis=axis) for parts, axis in zip(zip(*halves), (3, 1, 0, 1, 0))
  )
  early = (g_first, g_first_bias, g_second, g_second_bias)
  mixed = back_lon(banded, back_cos[recv_m], back_sin[recv_m]).reshape(fields.shape)
  block_output = (fields.astype(jnp.float32) + scaled.astype(jnp.float32) + mixed).astype(
      jnp.bfloat16
  )
  grad_scaled = cotangent.astype(jnp.float32) + back_lon(
      grad_banded, ahead_cos[recv_m], ahead_sin[recv_m]
  ).reshape(fields.shape)
  grad_fields = (
      cotangent.astype(jnp.float32)
      + norm_backward(grad_scaled, normed, inverse_std, norm_gain)
  ).astype(jnp.bfloat16)
  g_gain = jnp.sum(grad_scaled * normed, axis=(0, 1, 2))
  g_shift = jnp.sum(grad_scaled, axis=(0, 1, 2))
  late = allsum_small(jnp.stack([g_gain, g_shift]))
  token_total = lax.axis_size("dp") * samples * LAT * LON
  scale = 1.0 / math.sqrt(token_total)
  return (block_output, grad_fields) + tuple(part * scale for part in early) + (
      late[0] * scale,
      late[1] * scale,
  )


def psum_flat(parts):
    flat = jnp.concatenate([part.reshape(-1) for part in parts])
    size = flat.shape[0]
    unit = 1024 * lax.axis_size("dp")
    padded = -(-size // unit) * unit
    flat = jnp.pad(flat, (0, padded - size)).reshape(padded // 128, 128)
    flat = allsum_large(flat).reshape(-1)
    pieces, offset = [], 0
    for part in parts:
        pieces.append(flat[offset : offset + part.size].reshape(part.shape))
        offset += part.size
    return tuple(pieces)


def allsum_large(values):
    n = lax.axis_size("dp")
    if n & (n - 1):
        return lax.psum(values, ("dp", "spatial"))
    me = lax.axis_index("dp")
    bits = []
    step = 1
    while step < n:
        bits.append(step)
        step *= 2
    for step in bits:
        half = values.shape[0] // 2
        high = (me // step) % 2
        keep = lax.dynamic_slice_in_dim(values, high * half, half, axis=0)
        send = lax.dynamic_slice_in_dim(values, (1 - high) * half, half, axis=0)
        values = keep + lax.ppermute(send, "dp", [(i, i ^ step) for i in range(n)])
    values = allsum_small(values, ("spatial",))
    for step in reversed(bits):
        high = (me // step) % 2
        other = lax.ppermute(values, "dp", [(i, i ^ step) for i in range(n)])
        values = jnp.where(
            high == 0,
            jnp.concatenate([values, other], axis=0),
            jnp.concatenate([other, values], axis=0),
        )
    return values


def solution(mesh):
    return jax.shard_map(
        local,
        mesh=mesh,
        in_specs=(
            P("dp", "spatial", None, None),
            P(),
            P(),
            P(),
            P(),
            P(),
            P(),
            P("dp", "spatial", None, None),
        ),
        out_specs=(
            P("dp", "spatial", None, None),
            P("dp", "spatial", None, None),
            P(),
            P(),
            P(),
            P(),
            P(),
            P(),
        ),
        check_vma=False,
    )
```

```python
import math

import jax
import jax.numpy as jnp
from jax import lax
from jax.sharding import PartitionSpec as P


LAT = 64
LON = 128
BLOCKS = 8
BLOCK = 96


shrink_cut = 0.01
norm_epsilon = 1e-06
gelu_factor = 0.7978845608
gelu_cubic = 0.044715


def product(pattern, left_side, right_side):
    return jnp.einsum(pattern, left_side, right_side, preferred_element_type=jnp.float32)


def tables(count, mode_count, doubled):
    positions = jnp.arange(count, dtype=jnp.int32)
    orders = jnp.arange(mode_count, dtype=jnp.int32)
    phases = orders[:, None] * positions[None, :] % count
    angles = 2.0 * math.pi / count * phases.astype(jnp.float32)
    factor = jnp.ones((mode_count, 1), jnp.float32) / math.sqrt(count)
    if doubled:
        factor = factor * jnp.where(orders == 0, 1.0, 2.0).astype(jnp.float32)[:, None]
    return (
        (jnp.cos(angles) * factor).astype(jnp.bfloat16),
        (jnp.sin(angles) * factor).astype(jnp.bfloat16),
    )


def rotate(values):
    half_width = values.shape[-1] // 2
    return jnp.concatenate([values[..., half_width:], -values[..., :half_width]], axis=-1)


def along_lon(real_part, cos_table, sin_table):
    real_sum = product("bhwnp,mw->bhmnp", real_part, cos_table)
    imag_sum = -product("bhwnp,mw->bhmnp", real_part, sin_table)
    return jnp.concatenate([real_sum, imag_sum], axis=-1).astype(jnp.bfloat16)


def back_lon(spectral, cos_table, sin_table):
    half_width = spectral.shape[-1] // 2
    return product("bhmnp,mw->bhwnp", spectral[..., :half_width], cos_table) - product(
        "bhmnp,mw->bhwnp", spectral[..., half_width:], sin_table
    )


def along_lat(spectral, cos_table, sin_table):
    stacked = jnp.concatenate([spectral, rotate(spectral)], axis=1)
    table = jnp.concatenate([cos_table, sin_table], axis=1)
    return product("kh,bhmnp->bkmnp", table, stacked).astype(jnp.bfloat16)


def back_lat(spectral, cos_table, sin_table):
    stacked = jnp.concatenate([spectral, -rotate(spectral)], axis=1)
    table = jnp.concatenate([cos_table, sin_table], axis=1)
    return product("kh,bhmnp->bkmnp", table, stacked).astype(jnp.bfloat16)


def real_blocks(weight):
    upper_rows = jnp.concatenate([weight[0], weight[1]], axis=-1)
    bottom = jnp.concatenate([-weight[1], weight[0]], axis=-1)
    return jnp.concatenate([upper_rows, bottom], axis=1)


def fold_blocks(gradient):
    half_width = gradient.shape[-1] // 2
    real_grad = gradient[:, :half_width, :half_width] + gradient[:, half_width:, half_width:]
    imag_grad = gradient[:, :half_width, half_width:] - gradient[:, half_width:, :half_width]
    return jnp.stack([real_grad, imag_grad])


def gelu_value(values):
    inner = jnp.tanh(gelu_factor * (values + gelu_cubic * values * values * values))
    return 0.5 * values * (1.0 + inner)


def gelu_slope(values):
    inner = jnp.tanh(gelu_factor * (values + gelu_cubic * values * values * values))
    return 0.5 * (1.0 + inner) + 0.5 * values * (1.0 - inner * inner) * gelu_factor * (
        1.0 + 3.0 * gelu_cubic * values * values
    )


def spectral_forward(transformed, first_real, first_bias, second_real, second_bias):
    hidden_pre = product("bkmnp,npq->bkmnq", transformed, first_real) + first_bias
    hidden = gelu_value(hidden_pre).astype(jnp.bfloat16)
    output_pre = product("bkmnp,npq->bkmnq", hidden, second_real) + second_bias
    shrunk = (output_pre - shrink_cut * jnp.tanh(output_pre / shrink_cut)).astype(jnp.bfloat16)
    return (hidden_pre, hidden, output_pre, shrunk)


def spectral_backward(
    transformed, hidden_pre, hidden, output_pre, grad_shrunk, first_real, second_real
):
    bend = jnp.tanh(output_pre / shrink_cut)
    grad_outpre = (grad_shrunk.astype(jnp.float32) * bend * bend).astype(jnp.bfloat16)
    grad_second = product("bkmnp,bkmnq->npq", hidden, grad_outpre)
    grad_second_bias = jnp.sum(grad_outpre.astype(jnp.float32), axis=(0, 1, 2))
    grad_hidden = product("bkmnq,npq->bkmnp", grad_outpre, second_real)
    grad_hidpre = (grad_hidden * gelu_slope(hidden_pre)).astype(jnp.bfloat16)
    grad_first = product("bkmnp,bkmnq->npq", transformed, grad_hidpre)
    grad_first_bias = jnp.sum(grad_hidpre.astype(jnp.float32), axis=(0, 1, 2))
    grad_transformed = product("bkmnq,npq->bkmnp", grad_hidpre, first_real).astype(jnp.bfloat16)
    return (grad_transformed, grad_first, grad_first_bias, grad_second, grad_second_bias)


def normalize(fields):
    values = fields.astype(jnp.float32)
    center = jnp.mean(values, axis=-1, keepdims=True)
    spread = jnp.mean((values - center) ** 2, axis=-1, keepdims=True)
    inverse_std = lax.rsqrt(spread + norm_epsilon)
    return ((values - center) * inverse_std, inverse_std)


def norm_backward(grad_scaled, normed, inverse_std, norm_gain):
    grad_normed = grad_scaled * norm_gain
    mean_grad = jnp.mean(grad_normed, axis=-1, keepdims=True)
    mean_cross = jnp.mean(grad_normed * normed, axis=-1, keepdims=True)
    return inverse_std * (grad_normed - mean_grad - normed * mean_cross)


def send_order(me, n, size):
    chunk = (me + jnp.arange(n, dtype=jnp.int32)[:, None]) % n
    return (chunk * size + jnp.arange(size, dtype=jnp.int32)[None, :]).reshape(-1)


def receive_order(me, n, size):
    chunk = (me + n - jnp.arange(n, dtype=jnp.int32)[:, None]) % n
    return (chunk * size + jnp.arange(size, dtype=jnp.int32)[None, :]).reshape(-1)


def exchange(values, split_axis, concat_axis):
    n = lax.axis_size("spatial")
    size = values.shape[split_axis] // n
    pieces = [lax.slice_in_dim(values, k * size, (k + 1) * size, axis=split_axis) for k in range(n)]
    received = [pieces[0]] + [
        lax.ppermute(pieces[k], "spatial", [(i, (i + k) % n) for i in range(n)])
        for k in range(1, n)
    ]
    return jnp.concatenate(received, axis=concat_axis)


def allsum_small(values, axes=("spatial", "dp")):
    for axis in axes:
        n = lax.axis_size(axis)
        if n & (n - 1):
            values = lax.psum(values, axis)
            continue
        step = 1
        while step < n:
            values = values + lax.ppermute(values, axis, [(i, i ^ step) for i in range(n)])
            step *= 2
    return values


def local(
    fields, norm_gain, norm_shift, first_weight, first_bias, second_weight, second_bias, cotangent
):
  samples, band_rows, longitudes, _ = fields.shape
  mode_count = longitudes // 2
  n = lax.axis_size("spatial")
  me = lax.axis_index("spatial")
  modes_per = mode_count // n
  send_m = send_order(me, n, modes_per)
  recv_m = receive_order(me, n, modes_per)
  send_h = send_order(me, n, band_rows)
  recv_h = receive_order(me, n, band_rows)
  ahead_cos, ahead_sin = tables(longitudes, mode_count, False)
  back_cos, back_sin = tables(longitudes, mode_count, True)
  polar_cos, polar_sin = tables(LAT, LAT, False)
  first_real = real_blocks(first_weight)
  second_real = real_blocks(second_weight)
  block_shape = (samples, band_rows, longitudes, BLOCKS, BLOCK)
  normed, inverse_std = normalize(fields)
  scaled = (normed * norm_gain + norm_shift).astype(jnp.bfloat16)
  spectral = along_lon(scaled.reshape(block_shape), ahead_cos[send_m], ahead_sin[send_m])
  columns = exchange(spectral, 2, 1)
  grad_returned = along_lon(cotangent.reshape(block_shape), back_cos[send_m], back_sin[send_m])
  grad_columns = exchange(grad_returned, 2, 1)
  forward = []
  for lo, hi in ((0, BLOCKS // 2), (BLOCKS // 2, BLOCKS)):
      transformed = along_lat(columns[:, :, :, lo:hi], polar_cos[:, recv_h], polar_sin[:, recv_h])
      hidden_pre, hidden, output_pre, shrunk = spectral_forward(
          transformed, first_real[lo:hi], first_bias[lo:hi], second_real[lo:hi], second_bias[lo:hi]
      )
      returned = back_lat(shrunk, polar_cos[send_h], polar_sin[send_h])
      banded = exchange(returned, 1, 2)
      forward.append((banded, transformed, hidden_pre, hidden, output_pre))
  halves = []
  for half, (lo, hi) in enumerate(((0, BLOCKS // 2), (BLOCKS // 2, BLOCKS))):
      _, transformed, hidden_pre, hidden, output_pre = forward[half]
      grad_shrunk = along_lat(
          grad_columns[:, :, :, lo:hi], polar_cos[:, recv_h], polar_sin[:, recv_h]
      )
      grad_transformed, g_first, g_first_bias, g_second, g_second_bias = spectral_backward(
          transformed,
          hidden_pre,
          hidden,
          output_pre,
          grad_shrunk,
          first_real[lo:hi],
          second_real[lo:hi],
      )
      grad_spectral = back_lat(grad_transformed, polar_cos[send_h], polar_sin[send_h])
      grad_banded = exchange(grad_spectral, 1, 2)
      halves.append((grad_banded, g_first, g_first_bias, g_second, g_second_bias))
  banded = jnp.concatenate([part[0] for part in forward], axis=3)
  grad_banded, g_first, g_first_bias, g_second, g_second_bias = (
      jnp.concatenate(parts, axis=axis) for parts, axis in zip(zip(*halves), (3, 0, 0, 0, 0))
  )
  early = psum_flat((fold_blocks(g_first), g_first_bias, fold_blocks(g_second), g_second_bias))
  mixed = back_lon(banded, back_cos[recv_m], back_sin[recv_m]).reshape(fields.shape)
  block_output = (fields.astype(jnp.float32) + scaled.astype(jnp.float32) + mixed).astype(
      jnp.bfloat16
  )
  grad_scaled = cotangent.astype(jnp.float32) + back_lon(
      grad_banded, ahead_cos[recv_m], ahead_sin[recv_m]
  ).reshape(fields.shape)
  grad_fields = (
      cotangent.astype(jnp.float32) + norm_backward(grad_scaled, normed, inverse_std, norm_gain)
  ).astype(jnp.bfloat16)
  g_gain = jnp.sum(grad_scaled * normed, axis=(0, 1, 2))
  g_shift = jnp.sum(grad_scaled, axis=(0, 1, 2))
  late = allsum_small(jnp.stack([g_gain, g_shift]))
  token_total = lax.axis_size("dp") * samples * LAT * LON
  scale = 1.0 / math.sqrt(token_total)
  return (block_output, grad_fields) + tuple(part * scale for part in early) + (
      late[0] * scale,
      late[1] * scale,
  )


def psum_flat(parts):
    flat = jnp.concatenate([part.reshape(-1) for part in parts])
    size = flat.shape[0]
    unit = 1024 * lax.axis_size("dp")
    padded = -(-size // unit) * unit
    flat = jnp.pad(flat, (0, padded - size)).reshape(padded // 128, 128)
    flat = allsum_large(flat).reshape(-1)
    pieces, offset = [], 0
    for part in parts:
        pieces.append(flat[offset : offset + part.size].reshape(part.shape))
        offset += part.size
    return tuple(pieces)


def allsum_large(values):
    n = lax.axis_size("dp")
    if n & (n - 1):
        return lax.psum(values, ("dp", "spatial"))
    me = lax.axis_index("dp")
    bits = []
    step = 1
    while step < n:
        bits.append(step)
        step *= 2
    for step in bits:
        half = values.shape[0] // 2
        high = (me // step) % 2
        keep = lax.dynamic_slice_in_dim(values, high * half, half, axis=0)
        send = lax.dynamic_slice_in_dim(values, (1 - high) * half, half, axis=0)
        values = keep + lax.ppermute(send, "dp", [(i, i ^ step) for i in range(n)])
    values = allsum_small(values, ("spatial",))
    for step in reversed(bits):
        high = (me // step) % 2
        other = lax.ppermute(values, "dp", [(i, i ^ step) for i in range(n)])
        values = jnp.where(
            high == 0,
            jnp.concatenate([values, other], axis=0),
            jnp.concatenate([other, values], axis=0),
        )
    return values


def solution(mesh):
    return jax.shard_map(
        local,
        mesh=mesh,
        in_specs=(
            P("dp", "spatial", None, None),
            P(),
            P(),
            P(),
            P(),
            P(),
            P(),
            P("dp", "spatial", None, None),
        ),
        out_specs=(
            P("dp", "spatial", None, None),
            P("dp", "spatial", None, None),
            P(),
            P(),
            P(),
            P(),
            P(),
            P(),
        ),
        check_vma=False,
    )
```

```python
import math

import jax
import jax.numpy as jnp
from jax import lax
from jax.sharding import PartitionSpec as P


LAT = 64
LON = 128
BLOCKS = 8
BLOCK = 96


shrink_cut = 0.01
norm_epsilon = 1e-06
gelu_factor = 0.7978845608
gelu_cubic = 0.044715


def product(pattern, left_side, right_side):
    return jnp.einsum(pattern, left_side, right_side, preferred_element_type=jnp.float32)


def tables(count, mode_count, doubled):
    positions = jnp.arange(count, dtype=jnp.int32)
    orders = jnp.arange(mode_count, dtype=jnp.int32)
    phases = orders[:, None] * positions[None, :] % count
    angles = 2.0 * math.pi / count * phases.astype(jnp.float32)
    factor = jnp.ones((mode_count, 1), jnp.float32) / math.sqrt(count)
    if doubled:
        factor = factor * jnp.where(orders == 0, 1.0, 2.0).astype(jnp.float32)[:, None]
    return (
        (jnp.cos(angles) * factor).astype(jnp.bfloat16),
        (jnp.sin(angles) * factor).astype(jnp.bfloat16),
    )


def rotate(values):
    half_width = values.shape[-1] // 2
    return jnp.concatenate([values[..., half_width:], -values[..., :half_width]], axis=-1)


def along_lon(real_part, cos_table, sin_table):
    real_sum = product("bhwnp,mw->bhmnp", real_part, cos_table)
    imag_sum = -product("bhwnp,mw->bhmnp", real_part, sin_table)
    return jnp.concatenate([real_sum, imag_sum], axis=-1).astype(jnp.bfloat16)


def back_lon(spectral, cos_table, sin_table):
    half_width = spectral.shape[-1] // 2
    return product("bhmnp,mw->bhwnp", spectral[..., :half_width], cos_table) - product(
        "bhmnp,mw->bhwnp", spectral[..., half_width:], sin_table
    )


def along_lat(spectral, cos_table, sin_table):
    stacked = jnp.concatenate([spectral, rotate(spectral)], axis=1)
    table = jnp.concatenate([cos_table, sin_table], axis=1)
    return product("kh,bhmnp->bkmnp", table, stacked).astype(jnp.bfloat16)


def back_lat(spectral, cos_table, sin_table):
    stacked = jnp.concatenate([spectral, -rotate(spectral)], axis=1)
    table = jnp.concatenate([cos_table, sin_table], axis=1)
    return product("kh,bhmnp->bkmnp", table, stacked).astype(jnp.bfloat16)


def real_blocks(weight):
    upper_rows = jnp.concatenate([weight[0], weight[1]], axis=-1)
    bottom = jnp.concatenate([-weight[1], weight[0]], axis=-1)
    return jnp.concatenate([upper_rows, bottom], axis=1)


def fold_blocks(gradient):
    half_width = gradient.shape[-1] // 2
    real_grad = gradient[:, :half_width, :half_width] + gradient[:, half_width:, half_width:]
    imag_grad = gradient[:, :half_width, half_width:] - gradient[:, half_width:, :half_width]
    return jnp.stack([real_grad, imag_grad])


def gelu_value(values):
    inner = jnp.tanh(gelu_factor * (values + gelu_cubic * values * values * values))
    return 0.5 * values * (1.0 + inner)


def gelu_slope(values):
    inner = jnp.tanh(gelu_factor * (values + gelu_cubic * values * values * values))
    return 0.5 * (1.0 + inner) + 0.5 * values * (1.0 - inner * inner) * gelu_factor * (
        1.0 + 3.0 * gelu_cubic * values * values
    )


def spectral_forward(transformed, first_real, first_bias, second_real, second_bias):
    hidden_pre = product("bkmnp,npq->bkmnq", transformed, first_real) + first_bias
    hidden = gelu_value(hidden_pre).astype(jnp.bfloat16)
    output_pre = product("bkmnp,npq->bkmnq", hidden, second_real) + second_bias
    shrunk = (output_pre - shrink_cut * jnp.tanh(output_pre / shrink_cut)).astype(jnp.bfloat16)
    return (hidden_pre, hidden, output_pre, shrunk)


def spectral_backward(
    transformed, hidden_pre, hidden, output_pre, grad_shrunk, first_real, second_real
):
    bend = jnp.tanh(output_pre / shrink_cut)
    grad_outpre = (grad_shrunk.astype(jnp.float32) * bend * bend).astype(jnp.bfloat16)
    grad_second = product("bkmnp,bkmnq->npq", hidden, grad_outpre)
    grad_second_bias = jnp.sum(grad_outpre.astype(jnp.float32), axis=(0, 1, 2))
    grad_hidden = product("bkmnq,npq->bkmnp", grad_outpre, second_real)
    grad_hidpre = (grad_hidden * gelu_slope(hidden_pre)).astype(jnp.bfloat16)
    grad_first = product("bkmnp,bkmnq->npq", transformed, grad_hidpre)
    grad_first_bias = jnp.sum(grad_hidpre.astype(jnp.float32), axis=(0, 1, 2))
    grad_transformed = product("bkmnq,npq->bkmnp", grad_hidpre, first_real).astype(jnp.bfloat16)
    return (grad_transformed, grad_first, grad_first_bias, grad_second, grad_second_bias)


def normalize(fields):
    values = fields.astype(jnp.float32)
    center = jnp.mean(values, axis=-1, keepdims=True)
    spread = jnp.mean((values - center) ** 2, axis=-1, keepdims=True)
    inverse_std = lax.rsqrt(spread + norm_epsilon)
    return ((values - center) * inverse_std, inverse_std)


def norm_backward(grad_scaled, normed, inverse_std, norm_gain):
    grad_normed = grad_scaled * norm_gain
    mean_grad = jnp.mean(grad_normed, axis=-1, keepdims=True)
    mean_cross = jnp.mean(grad_normed * normed, axis=-1, keepdims=True)
    return inverse_std * (grad_normed - mean_grad - normed * mean_cross)


def send_order(me, n, size):
    chunk = (me + jnp.arange(n, dtype=jnp.int32)[:, None]) % n
    return (chunk * size + jnp.arange(size, dtype=jnp.int32)[None, :]).reshape(-1)


def receive_order(me, n, size):
    chunk = (me + n - jnp.arange(n, dtype=jnp.int32)[:, None]) % n
    return (chunk * size + jnp.arange(size, dtype=jnp.int32)[None, :]).reshape(-1)


def exchange(values, split_axis, concat_axis):
    n = lax.axis_size("spatial")
    size = values.shape[split_axis] // n
    pieces = [lax.slice_in_dim(values, k * size, (k + 1) * size, axis=split_axis) for k in range(n)]
    received = [pieces[0]] + [
        lax.ppermute(pieces[k], "spatial", [(i, (i + k) % n) for i in range(n)])
        for k in range(1, n)
    ]
    return jnp.concatenate(received, axis=concat_axis)


def allsum_small(values, axes=("spatial", "dp")):
    for axis in axes:
        n = lax.axis_size(axis)
        if n & (n - 1):
            values = lax.psum(values, axis)
            continue
        step = 1
        while step < n:
            values = values + lax.ppermute(values, axis, [(i, i ^ step) for i in range(n)])
            step *= 2
    return values


def local(
    fields, norm_gain, norm_shift, first_weight, first_bias, second_weight, second_bias, cotangent
):
  samples, band_rows, longitudes, _ = fields.shape
  mode_count = longitudes // 2
  n = lax.axis_size("spatial")
  me = lax.axis_index("spatial")
  modes_per = mode_count // n
  send_m = send_order(me, n, modes_per)
  recv_m = receive_order(me, n, modes_per)
  send_h = send_order(me, n, band_rows)
  recv_h = receive_order(me, n, band_rows)
  ahead_cos, ahead_sin = tables(longitudes, mode_count, False)
  back_cos, back_sin = tables(longitudes, mode_count, True)
  polar_cos, polar_sin = tables(LAT, LAT, False)
  first_real = real_blocks(first_weight)
  second_real = real_blocks(second_weight)
  block_shape = (samples, band_rows, longitudes, BLOCKS, BLOCK)
  normed, inverse_std = normalize(fields)
  scaled = (normed * norm_gain + norm_shift).astype(jnp.bfloat16)
  spectral = along_lon(scaled.reshape(block_shape), ahead_cos[send_m], ahead_sin[send_m])
  columns = exchange(spectral, 2, 1)
  grad_returned = along_lon(cotangent.reshape(block_shape), back_cos[send_m], back_sin[send_m])
  grad_columns = exchange(grad_returned, 2, 1)
  transformed = along_lat(columns, polar_cos[:, recv_h], polar_sin[:, recv_h])
  hidden_pre, hidden, output_pre, shrunk = spectral_forward(
      transformed, first_real, first_bias, second_real, second_bias
  )
  returned = back_lat(shrunk, polar_cos[send_h], polar_sin[send_h])
  banded = exchange(returned, 1, 2)
  halves = []
  for lo, hi in ((0, BLOCKS // 2), (BLOCKS // 2, BLOCKS)):
      pick = lambda values: values[:, :, :, lo:hi]
      grad_shrunk = along_lat(pick(grad_columns), polar_cos[:, recv_h], polar_sin[:, recv_h])
      grad_transformed, g_first, g_first_bias, g_second, g_second_bias = spectral_backward(
          pick(transformed),
          pick(hidden_pre),
          pick(hidden),
          pick(output_pre),
          grad_shrunk,
          first_real[lo:hi],
          second_real[lo:hi],
      )
      grad_spectral = back_lat(grad_transformed, polar_cos[send_h], polar_sin[send_h])
      grad_banded = exchange(grad_spectral, 1, 2)
      halves.append((grad_banded, g_first, g_first_bias, g_second, g_second_bias))
  grad_banded, g_first, g_first_bias, g_second, g_second_bias = (
      jnp.concatenate(parts, axis=axis) for parts, axis in zip(zip(*halves), (3, 0, 0, 0, 0))
  )
  weight_parts = (fold_blocks(g_first), g_first_bias, fold_blocks(g_second), g_second_bias)
  owned = scatter_dp(flatten(weight_parts))
  mixed = back_lon(banded, back_cos[recv_m], back_sin[recv_m]).reshape(fields.shape)
  block_output = (fields.astype(jnp.float32) + scaled.astype(jnp.float32) + mixed).astype(
      jnp.bfloat16
  )
  grad_scaled = cotangent.astype(jnp.float32) + back_lon(
      grad_banded, ahead_cos[recv_m], ahead_sin[recv_m]
  ).reshape(fields.shape)
  grad_fields = (
      cotangent.astype(jnp.float32) + norm_backward(grad_scaled, normed, inverse_std, norm_gain)
  ).astype(jnp.bfloat16)
  g_gain = jnp.sum(grad_scaled * normed, axis=(0, 1, 2))
  g_shift = jnp.sum(grad_scaled, axis=(0, 1, 2))
  weights, late = finish_sums(owned, jnp.stack([g_gain, g_shift]))
  early = unflatten(weights, weight_parts)
  token_total = lax.axis_size("dp") * samples * LAT * LON
  scale = 1.0 / math.sqrt(token_total)
  return (block_output, grad_fields) + tuple(part * scale for part in early) + (
      late[0] * scale,
      late[1] * scale,
  )


def flatten(parts):
    flat = jnp.concatenate([part.reshape(-1) for part in parts])
    size = flat.shape[0]
    unit = 1024 * lax.axis_size("dp")
    padded = -(-size // unit) * unit
    return jnp.pad(flat, (0, padded - size)).reshape(padded // 128, 128)


def unflatten(flat, parts):
    flat = flat.reshape(-1)
    pieces, offset = [], 0
    for part in parts:
        pieces.append(flat[offset : offset + part.size].reshape(part.shape))
        offset += part.size
    return tuple(pieces)


def dp_bits():
    n = lax.axis_size("dp")
    bits = []
    step = 1
    while step < n:
        bits.append(step)
        step *= 2
    return bits


def scatter_dp(values):
    n = lax.axis_size("dp")
    me = lax.axis_index("dp")
    for step in dp_bits():
        half = values.shape[0] // 2
        high = (me // step) % 2
        keep = lax.dynamic_slice_in_dim(values, high * half, half, axis=0)
        send = lax.dynamic_slice_in_dim(values, (1 - high) * half, half, axis=0)
        values = keep + lax.ppermute(send, "dp", [(i, i ^ step) for i in range(n)])
    return values


def gather_dp(values):
    n = lax.axis_size("dp")
    me = lax.axis_index("dp")
    for step in reversed(dp_bits()):
        high = (me // step) % 2
        other = lax.ppermute(values, "dp", [(i, i ^ step) for i in range(n)])
        values = jnp.where(
            high == 0,
            jnp.concatenate([values, other], axis=0),
            jnp.concatenate([other, values], axis=0),
        )
    return values


def finish_sums(owned, extra):
    n = lax.axis_size("dp")
    rows = owned.shape[0]
    extra_rows = -(-extra.size // 1024) * 8
    tail = jnp.pad(extra.reshape(-1), (0, extra_rows * 128 - extra.size))
    combined = jnp.concatenate([owned, tail.reshape(extra_rows, 128)], axis=0)
    combined = allsum_small(combined, ("spatial",))
    gathered = gather_dp(combined).reshape(n, rows + extra_rows, 128)
    weights = gathered[:, :rows].reshape(n * rows, 128)
    extra_sum = jnp.sum(gathered[:, rows:], axis=0).reshape(-1)[: extra.size]
    return weights, extra_sum.reshape(extra.shape)


def solution(mesh):
    return jax.shard_map(
        local,
        mesh=mesh,
        in_specs=(
            P("dp", "spatial", None, None),
            P(),
            P(),
            P(),
            P(),
            P(),
            P(),
            P("dp", "spatial", None, None),
        ),
        out_specs=(
            P("dp", "spatial", None, None),
            P("dp", "spatial", None, None),
            P(),
            P(),
            P(),
            P(),
            P(),
            P(),
        ),
        check_vma=False,
    )
```

```python
import math

import jax
import jax.numpy as jnp
from jax import lax
from jax.sharding import PartitionSpec as P


LAT = 64
LON = 128
BLOCKS = 8
BLOCK = 96


shrink_cut = 0.01
norm_epsilon = 1e-06
gelu_factor = 0.7978845608
gelu_cubic = 0.044715


def product(pattern, left_side, right_side):
    return jnp.einsum(pattern, left_side, right_side, preferred_element_type=jnp.float32)


def tables(count, mode_count, doubled):
    positions = jnp.arange(count, dtype=jnp.int32)
    orders = jnp.arange(mode_count, dtype=jnp.int32)
    phases = orders[:, None] * positions[None, :] % count
    angles = 2.0 * math.pi / count * phases.astype(jnp.float32)
    factor = jnp.ones((mode_count, 1), jnp.float32) / math.sqrt(count)
    if doubled:
        factor = factor * jnp.where(orders == 0, 1.0, 2.0).astype(jnp.float32)[:, None]
    return (
        (jnp.cos(angles) * factor).astype(jnp.bfloat16),
        (jnp.sin(angles) * factor).astype(jnp.bfloat16),
    )


def rotate(values):
    half_width = values.shape[-1] // 2
    return jnp.concatenate([values[..., half_width:], -values[..., :half_width]], axis=-1)


def along_lon(real_part, cos_table, sin_table):
    real_sum = product("bhwnp,mw->bhmnp", real_part, cos_table)
    imag_sum = -product("bhwnp,mw->bhmnp", real_part, sin_table)
    return jnp.concatenate([real_sum, imag_sum], axis=-1).astype(jnp.bfloat16)


def back_lon(spectral, cos_table, sin_table):
    half_width = spectral.shape[-1] // 2
    return product("bhmnp,mw->bhwnp", spectral[..., :half_width], cos_table) - product(
        "bhmnp,mw->bhwnp", spectral[..., half_width:], sin_table
    )


def along_lat(spectral, cos_table, sin_table):
    stacked = jnp.concatenate([spectral, rotate(spectral)], axis=1)
    table = jnp.concatenate([cos_table, sin_table], axis=1)
    return product("kh,bhmnp->bkmnp", table, stacked).astype(jnp.bfloat16)


def back_lat(spectral, cos_table, sin_table):
    stacked = jnp.concatenate([spectral, -rotate(spectral)], axis=1)
    table = jnp.concatenate([cos_table, sin_table], axis=1)
    return product("kh,bhmnp->bkmnp", table, stacked).astype(jnp.bfloat16)


def real_blocks(weight):
    upper_rows = jnp.concatenate([weight[0], weight[1]], axis=-1)
    bottom = jnp.concatenate([-weight[1], weight[0]], axis=-1)
    return jnp.concatenate([upper_rows, bottom], axis=1)


def fold_blocks(gradient):
    half_width = gradient.shape[-1] // 2
    real_grad = gradient[:, :half_width, :half_width] + gradient[:, half_width:, half_width:]
    imag_grad = gradient[:, :half_width, half_width:] - gradient[:, half_width:, :half_width]
    return jnp.stack([real_grad, imag_grad])


def gelu_value(values):
    inner = jnp.tanh(gelu_factor * (values + gelu_cubic * values * values * values))
    return 0.5 * values * (1.0 + inner)


def gelu_slope(values):
    inner = jnp.tanh(gelu_factor * (values + gelu_cubic * values * values * values))
    return 0.5 * (1.0 + inner) + 0.5 * values * (1.0 - inner * inner) * gelu_factor * (
        1.0 + 3.0 * gelu_cubic * values * values
    )


def spectral_forward(transformed, first_real, first_bias, second_real, second_bias):
    hidden_pre = product("bkmnp,npq->bkmnq", transformed, first_real) + first_bias
    hidden = gelu_value(hidden_pre).astype(jnp.bfloat16)
    output_pre = product("bkmnp,npq->bkmnq", hidden, second_real) + second_bias
    shrunk = (output_pre - shrink_cut * jnp.tanh(output_pre / shrink_cut)).astype(jnp.bfloat16)
    return (hidden_pre, hidden, output_pre, shrunk)


def spectral_backward(
    transformed, hidden_pre, hidden, output_pre, grad_shrunk, first_real, second_real
):
    bend = jnp.tanh(output_pre / shrink_cut)
    grad_outpre = (grad_shrunk.astype(jnp.float32) * bend * bend).astype(jnp.bfloat16)
    grad_second = product("bkmnp,bkmnq->npq", hidden, grad_outpre)
    grad_second_bias = jnp.sum(grad_outpre.astype(jnp.float32), axis=(0, 1, 2))
    grad_hidden = product("bkmnq,npq->bkmnp", grad_outpre, second_real)
    grad_hidpre = (grad_hidden * gelu_slope(hidden_pre)).astype(jnp.bfloat16)
    grad_first = product("bkmnp,bkmnq->npq", transformed, grad_hidpre)
    grad_first_bias = jnp.sum(grad_hidpre.astype(jnp.float32), axis=(0, 1, 2))
    grad_transformed = product("bkmnq,npq->bkmnp", grad_hidpre, first_real).astype(jnp.bfloat16)
    return (grad_transformed, grad_first, grad_first_bias, grad_second, grad_second_bias)


def normalize(fields):
    values = fields.astype(jnp.float32)
    center = jnp.mean(values, axis=-1, keepdims=True)
    spread = jnp.mean((values - center) ** 2, axis=-1, keepdims=True)
    inverse_std = lax.rsqrt(spread + norm_epsilon)
    return ((values - center) * inverse_std, inverse_std)


def norm_backward(grad_scaled, normed, inverse_std, norm_gain):
    grad_normed = grad_scaled * norm_gain
    mean_grad = jnp.mean(grad_normed, axis=-1, keepdims=True)
    mean_cross = jnp.mean(grad_normed * normed, axis=-1, keepdims=True)
    return inverse_std * (grad_normed - mean_grad - normed * mean_cross)


def send_order(me, n, size):
    chunk = (me + jnp.arange(n, dtype=jnp.int32)[:, None]) % n
    return (chunk * size + jnp.arange(size, dtype=jnp.int32)[None, :]).reshape(-1)


def receive_order(me, n, size):
    chunk = (me + n - jnp.arange(n, dtype=jnp.int32)[:, None]) % n
    return (chunk * size + jnp.arange(size, dtype=jnp.int32)[None, :]).reshape(-1)


def exchange(values, split_axis, concat_axis):
    n = lax.axis_size("spatial")
    size = values.shape[split_axis] // n
    pieces = [lax.slice_in_dim(values, k * size, (k + 1) * size, axis=split_axis) for k in range(n)]
    received = [pieces[0]] + [
        lax.ppermute(pieces[k], "spatial", [(i, (i + k) % n) for i in range(n)])
        for k in range(1, n)
    ]
    return jnp.concatenate(received, axis=concat_axis)


def allsum_small(values, axes=("spatial", "dp")):
    for axis in axes:
        n = lax.axis_size(axis)
        if n & (n - 1):
            values = lax.psum(values, axis)
            continue
        step = 1
        while step < n:
            values = values + lax.ppermute(values, axis, [(i, i ^ step) for i in range(n)])
            step *= 2
    return values


def local(
    fields, norm_gain, norm_shift, first_weight, first_bias, second_weight, second_bias, cotangent
):
  samples, band_rows, longitudes, _ = fields.shape
  mode_count = longitudes // 2
  n = lax.axis_size("spatial")
  me = lax.axis_index("spatial")
  modes_per = mode_count // n
  send_m = send_order(me, n, modes_per)
  recv_m = receive_order(me, n, modes_per)
  send_h = send_order(me, n, band_rows)
  recv_h = receive_order(me, n, band_rows)
  ahead_cos, ahead_sin = tables(longitudes, mode_count, False)
  back_cos, back_sin = tables(longitudes, mode_count, True)
  polar_cos, polar_sin = tables(LAT, LAT, False)
  first_real = real_blocks(first_weight)
  second_real = real_blocks(second_weight)
  block_shape = (samples, band_rows, longitudes, BLOCKS, BLOCK)
  normed, inverse_std = normalize(fields)
  scaled = (normed * norm_gain + norm_shift).astype(jnp.bfloat16)
  scaled_blocks = scaled.reshape(block_shape)
  sent = []
  for lo, hi in ((0, BLOCKS // 2), (BLOCKS // 2, BLOCKS)):
      spectral = along_lon(scaled_blocks[:, :, :, lo:hi], ahead_cos[send_m], ahead_sin[send_m])
      sent.append(exchange(spectral, 2, 1))
  columns = jnp.concatenate(sent, axis=3)
  grad_returned = along_lon(cotangent.reshape(block_shape), back_cos[send_m], back_sin[send_m])
  grad_columns = exchange(grad_returned, 2, 1)
  transformed = along_lat(columns, polar_cos[:, recv_h], polar_sin[:, recv_h])
  hidden_pre, hidden, output_pre, shrunk = spectral_forward(
      transformed, first_real, first_bias, second_real, second_bias
  )
  returned = back_lat(shrunk, polar_cos[send_h], polar_sin[send_h])
  banded = exchange(returned, 1, 2)
  halves = []
  for lo, hi in ((0, BLOCKS // 2), (BLOCKS // 2, BLOCKS)):
      pick = lambda values: values[:, :, :, lo:hi]
      grad_shrunk = along_lat(pick(grad_columns), polar_cos[:, recv_h], polar_sin[:, recv_h])
      grad_transformed, g_first, g_first_bias, g_second, g_second_bias = spectral_backward(
          pick(transformed),
          pick(hidden_pre),
          pick(hidden),
          pick(output_pre),
          grad_shrunk,
          first_real[lo:hi],
          second_real[lo:hi],
      )
      grad_spectral = back_lat(grad_transformed, polar_cos[send_h], polar_sin[send_h])
      grad_banded = exchange(grad_spectral, 1, 2)
      halves.append((grad_banded, g_first, g_first_bias, g_second, g_second_bias))
  grad_banded, g_first, g_first_bias, g_second, g_second_bias = (
      jnp.concatenate(parts, axis=axis) for parts, axis in zip(zip(*halves), (3, 0, 0, 0, 0))
  )
  early = psum_flat((fold_blocks(g_first), g_first_bias, fold_blocks(g_second), g_second_bias))
  mixed = back_lon(banded, back_cos[recv_m], back_sin[recv_m]).reshape(fields.shape)
  block_output = (fields.astype(jnp.float32) + scaled.astype(jnp.float32) + mixed).astype(
      jnp.bfloat16
  )
  grad_scaled = cotangent.astype(jnp.float32) + back_lon(
      grad_banded, ahead_cos[recv_m], ahead_sin[recv_m]
  ).reshape(fields.shape)
  grad_fields = (
      cotangent.astype(jnp.float32) + norm_backward(grad_scaled, normed, inverse_std, norm_gain)
  ).astype(jnp.bfloat16)
  g_gain = jnp.sum(grad_scaled * normed, axis=(0, 1, 2))
  g_shift = jnp.sum(grad_scaled, axis=(0, 1, 2))
  late = allsum_small(jnp.stack([g_gain, g_shift]))
  token_total = lax.axis_size("dp") * samples * LAT * LON
  scale = 1.0 / math.sqrt(token_total)
  return (block_output, grad_fields) + tuple(part * scale for part in early) + (
      late[0] * scale,
      late[1] * scale,
  )


def psum_flat(parts):
    flat = jnp.concatenate([part.reshape(-1) for part in parts])
    size = flat.shape[0]
    unit = 1024 * lax.axis_size("dp")
    padded = -(-size // unit) * unit
    flat = jnp.pad(flat, (0, padded - size)).reshape(padded // 128, 128)
    flat = allsum_large(flat).reshape(-1)
    pieces, offset = [], 0
    for part in parts:
        pieces.append(flat[offset : offset + part.size].reshape(part.shape))
        offset += part.size
    return tuple(pieces)


def allsum_large(values):
    n = lax.axis_size("dp")
    if n & (n - 1):
        return lax.psum(values, ("dp", "spatial"))
    me = lax.axis_index("dp")
    bits = []
    step = 1
    while step < n:
        bits.append(step)
        step *= 2
    for step in bits:
        half = values.shape[0] // 2
        high = (me // step) % 2
        keep = lax.dynamic_slice_in_dim(values, high * half, half, axis=0)
        send = lax.dynamic_slice_in_dim(values, (1 - high) * half, half, axis=0)
        values = keep + lax.ppermute(send, "dp", [(i, i ^ step) for i in range(n)])
    values = allsum_small(values, ("spatial",))
    for step in reversed(bits):
        high = (me // step) % 2
        other = lax.ppermute(values, "dp", [(i, i ^ step) for i in range(n)])
        values = jnp.where(
            high == 0,
            jnp.concatenate([values, other], axis=0),
            jnp.concatenate([other, values], axis=0),
        )
    return values


def solution(mesh):
    return jax.shard_map(
        local,
        mesh=mesh,
        in_specs=(
            P("dp", "spatial", None, None),
            P(),
            P(),
            P(),
            P(),
            P(),
            P(),
            P("dp", "spatial", None, None),
        ),
        out_specs=(
            P("dp", "spatial", None, None),
            P("dp", "spatial", None, None),
            P(),
            P(),
            P(),
            P(),
            P(),
            P(),
        ),
        check_vma=False,
    )
```

```python
import math

import jax
import jax.numpy as jnp
from jax import lax
from jax.sharding import PartitionSpec as P


LAT = 64
LON = 128
BLOCKS = 8
BLOCK = 96


shrink_cut = 0.01
norm_epsilon = 1e-06
gelu_factor = 0.7978845608
gelu_cubic = 0.044715


def product(pattern, left_side, right_side):
    return jnp.einsum(pattern, left_side, right_side, preferred_element_type=jnp.float32)


def tables(count, mode_count, doubled):
    positions = jnp.arange(count, dtype=jnp.int32)
    orders = jnp.arange(mode_count, dtype=jnp.int32)
    phases = orders[:, None] * positions[None, :] % count
    angles = 2.0 * math.pi / count * phases.astype(jnp.float32)
    factor = jnp.ones((mode_count, 1), jnp.float32) / math.sqrt(count)
    if doubled:
        factor = factor * jnp.where(orders == 0, 1.0, 2.0).astype(jnp.float32)[:, None]
    return (
        (jnp.cos(angles) * factor).astype(jnp.bfloat16),
        (jnp.sin(angles) * factor).astype(jnp.bfloat16),
    )


def rotate(values):
    half_width = values.shape[-1] // 2
    return jnp.concatenate([values[..., half_width:], -values[..., :half_width]], axis=-1)


def along_lon(real_part, cos_table, sin_table):
    real_sum = product("bhwnp,mw->bhmnp", real_part, cos_table)
    imag_sum = -product("bhwnp,mw->bhmnp", real_part, sin_table)
    return jnp.concatenate([real_sum, imag_sum], axis=-1).astype(jnp.bfloat16)


def back_lon(spectral, cos_table, sin_table):
    half_width = spectral.shape[-1] // 2
    return product("bhmnp,mw->bhwnp", spectral[..., :half_width], cos_table) - product(
        "bhmnp,mw->bhwnp", spectral[..., half_width:], sin_table
    )


def along_lat(spectral, cos_table, sin_table):
    stacked = jnp.concatenate([spectral, rotate(spectral)], axis=1)
    table = jnp.concatenate([cos_table, sin_table], axis=1)
    return product("kh,bhmnp->bkmnp", table, stacked).astype(jnp.bfloat16)


def back_lat(spectral, cos_table, sin_table):
    stacked = jnp.concatenate([spectral, -rotate(spectral)], axis=1)
    table = jnp.concatenate([cos_table, sin_table], axis=1)
    return product("kh,bhmnp->bkmnp", table, stacked).astype(jnp.bfloat16)


def real_blocks(weight):
    upper_rows = jnp.concatenate([weight[0], weight[1]], axis=-1)
    bottom = jnp.concatenate([-weight[1], weight[0]], axis=-1)
    return jnp.concatenate([upper_rows, bottom], axis=1)


def fold_blocks(gradient):
    half_width = gradient.shape[-1] // 2
    real_grad = gradient[:, :half_width, :half_width] + gradient[:, half_width:, half_width:]
    imag_grad = gradient[:, :half_width, half_width:] - gradient[:, half_width:, :half_width]
    return jnp.stack([real_grad, imag_grad])


def gelu_value(values):
    inner = jnp.tanh(gelu_factor * (values + gelu_cubic * values * values * values))
    return 0.5 * values * (1.0 + inner)


def gelu_slope(values):
    inner = jnp.tanh(gelu_factor * (values + gelu_cubic * values * values * values))
    return 0.5 * (1.0 + inner) + 0.5 * values * (1.0 - inner * inner) * gelu_factor * (
        1.0 + 3.0 * gelu_cubic * values * values
    )


def spectral_forward(transformed, first_real, first_bias, second_real, second_bias):
    hidden_pre = product("bkmnp,npq->bkmnq", transformed, first_real) + first_bias
    hidden = gelu_value(hidden_pre).astype(jnp.bfloat16)
    output_pre = product("bkmnp,npq->bkmnq", hidden, second_real) + second_bias
    shrunk = (output_pre - shrink_cut * jnp.tanh(output_pre / shrink_cut)).astype(jnp.bfloat16)
    return (hidden_pre, hidden, output_pre, shrunk)


def spectral_backward(
    transformed, hidden_pre, hidden, output_pre, grad_shrunk, first_real, second_real
):
    bend = jnp.tanh(output_pre / shrink_cut)
    grad_outpre = (grad_shrunk.astype(jnp.float32) * bend * bend).astype(jnp.bfloat16)
    grad_second = product("bkmnp,bkmnq->npq", hidden, grad_outpre)
    grad_second_bias = jnp.sum(grad_outpre.astype(jnp.float32), axis=(0, 1, 2))
    grad_hidden = product("bkmnq,npq->bkmnp", grad_outpre, second_real)
    grad_hidpre = (grad_hidden * gelu_slope(hidden_pre)).astype(jnp.bfloat16)
    grad_first = product("bkmnp,bkmnq->npq", transformed, grad_hidpre)
    grad_first_bias = jnp.sum(grad_hidpre.astype(jnp.float32), axis=(0, 1, 2))
    grad_transformed = product("bkmnq,npq->bkmnp", grad_hidpre, first_real).astype(jnp.bfloat16)
    return (grad_transformed, grad_first, grad_first_bias, grad_second, grad_second_bias)


def normalize(fields):
    values = fields.astype(jnp.float32)
    center = jnp.mean(values, axis=-1, keepdims=True)
    spread = jnp.mean((values - center) ** 2, axis=-1, keepdims=True)
    inverse_std = lax.rsqrt(spread + norm_epsilon)
    return ((values - center) * inverse_std, inverse_std)


def norm_backward(grad_scaled, normed, inverse_std, norm_gain):
    grad_normed = grad_scaled * norm_gain
    mean_grad = jnp.mean(grad_normed, axis=-1, keepdims=True)
    mean_cross = jnp.mean(grad_normed * normed, axis=-1, keepdims=True)
    return inverse_std * (grad_normed - mean_grad - normed * mean_cross)


def partner_order(me, n, size):
    chunk = jnp.bitwise_xor(me, jnp.arange(n, dtype=jnp.int32))[:, None]
    return (chunk * size + jnp.arange(size, dtype=jnp.int32)[None, :]).reshape(-1)


def exchange(values, split_axis, concat_axis):
    n = lax.axis_size("spatial")
    size = values.shape[split_axis] // n
    pieces = [lax.slice_in_dim(values, k * size, (k + 1) * size, axis=split_axis) for k in range(n)]
    received = [pieces[0]] + [None] * (n - 1)
    for k in sorted(range(1, n), key=lambda k: (k < 2, k)):
        received[k] = lax.ppermute(pieces[k], "spatial", [(i, i ^ k) for i in range(n)])
    return jnp.concatenate(received, axis=concat_axis)


def allsum_small(values, axes=("spatial", "dp")):
    for axis in axes:
        n = lax.axis_size(axis)
        if n & (n - 1):
            values = lax.psum(values, axis)
            continue
        step = 1
        while step < n:
            values = values + lax.ppermute(values, axis, [(i, i ^ step) for i in range(n)])
            step *= 2
    return values


def local(
    fields, norm_gain, norm_shift, first_weight, first_bias, second_weight, second_bias, cotangent
):
  samples, band_rows, longitudes, _ = fields.shape
  mode_count = longitudes // 2
  n = lax.axis_size("spatial")
  me = lax.axis_index("spatial")
  modes_per = mode_count // n
  send_m = partner_order(me, n, modes_per)
  recv_m = send_m
  send_h = partner_order(me, n, band_rows)
  recv_h = send_h
  ahead_cos, ahead_sin = tables(longitudes, mode_count, False)
  back_cos, back_sin = tables(longitudes, mode_count, True)
  polar_cos, polar_sin = tables(LAT, LAT, False)
  first_real = real_blocks(first_weight)
  second_real = real_blocks(second_weight)
  block_shape = (samples, band_rows, longitudes, BLOCKS, BLOCK)
  normed, inverse_std = normalize(fields)
  scaled = (normed * norm_gain + norm_shift).astype(jnp.bfloat16)
  spectral = along_lon(scaled.reshape(block_shape), ahead_cos[send_m], ahead_sin[send_m])
  columns = exchange(spectral, 2, 1)
  grad_returned = along_lon(cotangent.reshape(block_shape), back_cos[send_m], back_sin[send_m])
  grad_columns = exchange(grad_returned, 2, 1)
  transformed = along_lat(columns, polar_cos[:, recv_h], polar_sin[:, recv_h])
  hidden_pre, hidden, output_pre, shrunk = spectral_forward(
      transformed, first_real, first_bias, second_real, second_bias
  )
  returned = back_lat(shrunk, polar_cos[send_h], polar_sin[send_h])
  banded = exchange(returned, 1, 2)
  halves = []
  for lo, hi in ((0, BLOCKS // 2), (BLOCKS // 2, BLOCKS)):
      pick = lambda values: values[:, :, :, lo:hi]
      grad_shrunk = along_lat(pick(grad_columns), polar_cos[:, recv_h], polar_sin[:, recv_h])
      grad_transformed, g_first, g_first_bias, g_second, g_second_bias = spectral_backward(
          pick(transformed),
          pick(hidden_pre),
          pick(hidden),
          pick(output_pre),
          grad_shrunk,
          first_real[lo:hi],
          second_real[lo:hi],
      )
      grad_spectral = back_lat(grad_transformed, polar_cos[send_h], polar_sin[send_h])
      grad_banded = exchange(grad_spectral, 1, 2)
      halves.append((grad_banded, g_first, g_first_bias, g_second, g_second_bias))
  grad_banded, g_first, g_first_bias, g_second, g_second_bias = (
      jnp.concatenate(parts, axis=axis) for parts, axis in zip(zip(*halves), (3, 0, 0, 0, 0))
  )
  early = psum_flat((fold_blocks(g_first), g_first_bias, fold_blocks(g_second), g_second_bias))
  mixed = back_lon(banded, back_cos[recv_m], back_sin[recv_m]).reshape(fields.shape)
  block_output = (fields.astype(jnp.float32) + scaled.astype(jnp.float32) + mixed).astype(
      jnp.bfloat16
  )
  grad_scaled = cotangent.astype(jnp.float32) + back_lon(
      grad_banded, ahead_cos[recv_m], ahead_sin[recv_m]
  ).reshape(fields.shape)
  grad_fields = (
      cotangent.astype(jnp.float32) + norm_backward(grad_scaled, normed, inverse_std, norm_gain)
  ).astype(jnp.bfloat16)
  g_gain = jnp.sum(grad_scaled * normed, axis=(0, 1, 2))
  g_shift = jnp.sum(grad_scaled, axis=(0, 1, 2))
  late = allsum_small(jnp.stack([g_gain, g_shift]))
  token_total = lax.axis_size("dp") * samples * LAT * LON
  scale = 1.0 / math.sqrt(token_total)
  return (block_output, grad_fields) + tuple(part * scale for part in early) + (
      late[0] * scale,
      late[1] * scale,
  )


def psum_flat(parts):
    flat = jnp.concatenate([part.reshape(-1) for part in parts])
    size = flat.shape[0]
    unit = 1024 * lax.axis_size("dp")
    padded = -(-size // unit) * unit
    flat = jnp.pad(flat, (0, padded - size)).reshape(padded // 128, 128)
    flat = allsum_large(flat).reshape(-1)
    pieces, offset = [], 0
    for part in parts:
        pieces.append(flat[offset : offset + part.size].reshape(part.shape))
        offset += part.size
    return tuple(pieces)


def allsum_large(values):
    n = lax.axis_size("dp")
    if n & (n - 1):
        return lax.psum(values, ("dp", "spatial"))
    me = lax.axis_index("dp")
    bits = []
    step = 1
    while step < n:
        bits.append(step)
        step *= 2
    for step in bits:
        half = values.shape[0] // 2
        high = (me // step) % 2
        keep = lax.dynamic_slice_in_dim(values, high * half, half, axis=0)
        send = lax.dynamic_slice_in_dim(values, (1 - high) * half, half, axis=0)
        values = keep + lax.ppermute(send, "dp", [(i, i ^ step) for i in range(n)])
    values = allsum_small(values, ("spatial",))
    for step in reversed(bits):
        high = (me // step) % 2
        other = lax.ppermute(values, "dp", [(i, i ^ step) for i in range(n)])
        values = jnp.where(
            high == 0,
            jnp.concatenate([values, other], axis=0),
            jnp.concatenate([other, values], axis=0),
        )
    return values


def solution(mesh):
    return jax.shard_map(
        local,
        mesh=mesh,
        in_specs=(
            P("dp", "spatial", None, None),
            P(),
            P(),
            P(),
            P(),
            P(),
            P(),
            P("dp", "spatial", None, None),
        ),
        out_specs=(
            P("dp", "spatial", None, None),
            P("dp", "spatial", None, None),
            P(),
            P(),
            P(),
            P(),
            P(),
            P(),
        ),
        check_vma=False,
    )
```

```python
import math

import jax
import jax.numpy as jnp
from jax import lax
from jax.sharding import PartitionSpec as P


LAT = 64
LON = 128
BLOCKS = 8
BLOCK = 96


shrink_cut = 0.01
norm_epsilon = 1e-06
gelu_factor = 0.7978845608
gelu_cubic = 0.044715


def product(pattern, left_side, right_side):
    return jnp.einsum(pattern, left_side, right_side, preferred_element_type=jnp.float32)


def tables(count, mode_count, doubled):
    positions = jnp.arange(count, dtype=jnp.int32)
    orders = jnp.arange(mode_count, dtype=jnp.int32)
    phases = orders[:, None] * positions[None, :] % count
    angles = 2.0 * math.pi / count * phases.astype(jnp.float32)
    factor = jnp.ones((mode_count, 1), jnp.float32) / math.sqrt(count)
    if doubled:
        factor = factor * jnp.where(orders == 0, 1.0, 2.0).astype(jnp.float32)[:, None]
    return (
        (jnp.cos(angles) * factor).astype(jnp.bfloat16),
        (jnp.sin(angles) * factor).astype(jnp.bfloat16),
    )


def rotate(values):
    half_width = values.shape[-1] // 2
    return jnp.concatenate([values[..., half_width:], -values[..., :half_width]], axis=-1)


def along_lon(real_part, cos_table, sin_table):
    real_sum = product("bhwnp,mw->bhmnp", real_part, cos_table)
    imag_sum = -product("bhwnp,mw->bhmnp", real_part, sin_table)
    return jnp.concatenate([real_sum, imag_sum], axis=-1).astype(jnp.bfloat16)


def back_lon(spectral, cos_table, sin_table):
    half_width = spectral.shape[-1] // 2
    return product("bhmnp,mw->bhwnp", spectral[..., :half_width], cos_table) - product(
        "bhmnp,mw->bhwnp", spectral[..., half_width:], sin_table
    )


def along_lat(spectral, cos_table, sin_table):
    stacked = jnp.concatenate([spectral, rotate(spectral)], axis=1)
    table = jnp.concatenate([cos_table, sin_table], axis=1)
    return product("kh,bhmnp->bkmnp", table, stacked).astype(jnp.bfloat16)


def back_lat(spectral, cos_table, sin_table):
    stacked = jnp.concatenate([spectral, -rotate(spectral)], axis=1)
    table = jnp.concatenate([cos_table, sin_table], axis=1)
    return product("kh,bhmnp->bkmnp", table, stacked).astype(jnp.bfloat16)


def real_blocks(weight):
    upper_rows = jnp.concatenate([weight[0], weight[1]], axis=-1)
    bottom = jnp.concatenate([-weight[1], weight[0]], axis=-1)
    return jnp.concatenate([upper_rows, bottom], axis=1)


def fold_blocks(gradient):
    half_width = gradient.shape[-1] // 2
    real_grad = gradient[:, :half_width, :half_width] + gradient[:, half_width:, half_width:]
    imag_grad = gradient[:, :half_width, half_width:] - gradient[:, half_width:, :half_width]
    return jnp.stack([real_grad, imag_grad])


def gelu_value(values):
    inner = jnp.tanh(gelu_factor * (values + gelu_cubic * values * values * values))
    return 0.5 * values * (1.0 + inner)


def gelu_slope(values):
    inner = jnp.tanh(gelu_factor * (values + gelu_cubic * values * values * values))
    return 0.5 * (1.0 + inner) + 0.5 * values * (1.0 - inner * inner) * gelu_factor * (
        1.0 + 3.0 * gelu_cubic * values * values
    )


def spectral_forward(transformed, first_real, first_bias, second_real, second_bias):
    hidden_pre = product("bkmnp,npq->bkmnq", transformed, first_real) + first_bias
    hidden = gelu_value(hidden_pre).astype(jnp.bfloat16)
    output_pre = product("bkmnp,npq->bkmnq", hidden, second_real) + second_bias
    shrunk = (output_pre - shrink_cut * jnp.tanh(output_pre / shrink_cut)).astype(jnp.bfloat16)
    return (hidden_pre, hidden, output_pre, shrunk)


def spectral_backward(
    transformed, hidden_pre, hidden, output_pre, grad_shrunk, first_real, second_real
):
    bend = jnp.tanh(output_pre / shrink_cut)
    grad_outpre = (grad_shrunk.astype(jnp.float32) * bend * bend).astype(jnp.bfloat16)
    grad_second = product("bkmnp,bkmnq->npq", hidden, grad_outpre)
    grad_second_bias = jnp.sum(grad_outpre.astype(jnp.float32), axis=(0, 1, 2))
    grad_hidden = product("bkmnq,npq->bkmnp", grad_outpre, second_real)
    grad_hidpre = (grad_hidden * gelu_slope(hidden_pre)).astype(jnp.bfloat16)
    grad_first = product("bkmnp,bkmnq->npq", transformed, grad_hidpre)
    grad_first_bias = jnp.sum(grad_hidpre.astype(jnp.float32), axis=(0, 1, 2))
    grad_transformed = product("bkmnq,npq->bkmnp", grad_hidpre, first_real).astype(jnp.bfloat16)
    return (grad_transformed, grad_first, grad_first_bias, grad_second, grad_second_bias)


def normalize(fields):
    values = fields.astype(jnp.float32)
    center = jnp.mean(values, axis=-1, keepdims=True)
    spread = jnp.mean((values - center) ** 2, axis=-1, keepdims=True)
    inverse_std = lax.rsqrt(spread + norm_epsilon)
    return ((values - center) * inverse_std, inverse_std)


def norm_backward(grad_scaled, normed, inverse_std, norm_gain):
    grad_normed = grad_scaled * norm_gain
    mean_grad = jnp.mean(grad_normed, axis=-1, keepdims=True)
    mean_cross = jnp.mean(grad_normed * normed, axis=-1, keepdims=True)
    return inverse_std * (grad_normed - mean_grad - normed * mean_cross)


def send_order(me, n, size):
    chunk = (me + jnp.arange(n, dtype=jnp.int32)[:, None]) % n
    return (chunk * size + jnp.arange(size, dtype=jnp.int32)[None, :]).reshape(-1)


def receive_order(me, n, size):
    chunk = (me + n - jnp.arange(n, dtype=jnp.int32)[:, None]) % n
    return (chunk * size + jnp.arange(size, dtype=jnp.int32)[None, :]).reshape(-1)


def exchange(values, split_axis, concat_axis):
    n = lax.axis_size("spatial")
    size = values.shape[split_axis] // n
    pieces = [lax.slice_in_dim(values, k * size, (k + 1) * size, axis=split_axis) for k in range(n)]
    received = [pieces[0]] + [
        lax.ppermute(pieces[k], "spatial", [(i, (i + k) % n) for i in range(n)])
        for k in range(1, n)
    ]
    return jnp.concatenate(received, axis=concat_axis)


def allsum_small(values, axes=("spatial", "dp")):
    for axis in axes:
        n = lax.axis_size(axis)
        if n & (n - 1):
            values = lax.psum(values, axis)
            continue
        step = 1
        while step < n:
            values = values + lax.ppermute(values, axis, [(i, i ^ step) for i in range(n)])
            step *= 2
    return values


def local(
    fields, norm_gain, norm_shift, first_weight, first_bias, second_weight, second_bias, cotangent
):
  samples, band_rows, longitudes, _ = fields.shape
  mode_count = longitudes // 2
  n = lax.axis_size("spatial")
  me = lax.axis_index("spatial")
  modes_per = mode_count // n
  send_m = send_order(me, n, modes_per)
  recv_m = receive_order(me, n, modes_per)
  send_h = send_order(me, n, band_rows)
  recv_h = receive_order(me, n, band_rows)
  ahead_cos, ahead_sin = tables(longitudes, mode_count, False)
  back_cos, back_sin = tables(longitudes, mode_count, True)
  polar_cos, polar_sin = tables(LAT, LAT, False)
  first_real = real_blocks(first_weight)
  second_real = real_blocks(second_weight)
  block_shape = (samples, band_rows, longitudes, BLOCKS, BLOCK)
  normed, inverse_std = normalize(fields)
  scaled = (normed * norm_gain + norm_shift).astype(jnp.bfloat16)
  spectral = along_lon(scaled.reshape(block_shape), ahead_cos[send_m], ahead_sin[send_m])
  columns = exchange(spectral, 2, 1)
  grad_returned = along_lon(cotangent.reshape(block_shape), back_cos[send_m], back_sin[send_m])
  grad_columns = exchange(grad_returned, 2, 1)
  transformed = along_lat(columns, polar_cos[:, recv_h], polar_sin[:, recv_h])
  hidden_pre, hidden, output_pre, shrunk = spectral_forward(
      transformed, first_real, first_bias, second_real, second_bias
  )
  returned = back_lat(shrunk, polar_cos[send_h], polar_sin[send_h])
  banded = exchange(returned, 1, 2)
  halves = []
  for lo, hi in ((0, BLOCKS // 2), (BLOCKS // 2, BLOCKS)):
      pick = lambda values: values[:, :, :, lo:hi]
      grad_shrunk = along_lat(pick(grad_columns), polar_cos[:, recv_h], polar_sin[:, recv_h])
      grad_transformed, g_first, g_first_bias, g_second, g_second_bias = spectral_backward(
          pick(transformed),
          pick(hidden_pre),
          pick(hidden),
          pick(output_pre),
          grad_shrunk,
          first_real[lo:hi],
          second_real[lo:hi],
      )
      grad_spectral = back_lat(grad_transformed, polar_cos[send_h], polar_sin[send_h])
      grad_banded = exchange(grad_spectral, 1, 2)
      halves.append((grad_banded, g_first, g_first_bias, g_second, g_second_bias))
  grad_banded, g_first, g_first_bias, g_second, g_second_bias = (
      jnp.concatenate(parts, axis=axis) for parts, axis in zip(zip(*halves), (3, 0, 0, 0, 0))
  )
  early = psum_flat((fold_blocks(g_first), g_first_bias, fold_blocks(g_second), g_second_bias))
  mixed = back_lon(banded, back_cos[recv_m], back_sin[recv_m]).reshape(fields.shape)
  block_output = (fields.astype(jnp.float32) + scaled.astype(jnp.float32) + mixed).astype(
      jnp.bfloat16
  )
  grad_scaled = cotangent.astype(jnp.float32) + back_lon(
      grad_banded, ahead_cos[recv_m], ahead_sin[recv_m]
  ).reshape(fields.shape)
  grad_fields = (
      cotangent.astype(jnp.float32) + norm_backward(grad_scaled, normed, inverse_std, norm_gain)
  ).astype(jnp.bfloat16)
  g_gain = jnp.sum(grad_scaled * normed, axis=(0, 1, 2))
  g_shift = jnp.sum(grad_scaled, axis=(0, 1, 2))
  late = allsum_small(jnp.stack([g_gain, g_shift]))
  token_total = lax.axis_size("dp") * samples * LAT * LON
  scale = 1.0 / math.sqrt(token_total)
  return (block_output, grad_fields) + tuple(part * scale for part in early) + (
      late[0] * scale,
      late[1] * scale,
  )


def psum_flat(parts):
    rows = []
    for part in parts:
        width = -(-part.shape[-1] // 128) * 128
        pad = [(0, 0)] * (part.ndim - 1) + [(0, width - part.shape[-1])]
        rows.append(jnp.pad(part, pad).reshape(-1, 128))
    counts = [block.shape[0] for block in rows]
    flat = jnp.concatenate(rows, axis=0)
    unit = 8 * lax.axis_size("dp")
    padded = -(-flat.shape[0] // unit) * unit
    flat = allsum_large(jnp.pad(flat, ((0, padded - flat.shape[0]), (0, 0))))
    pieces, offset = [], 0
    for part, count in zip(parts, counts):
        width = -(-part.shape[-1] // 128) * 128
        block = flat[offset : offset + count].reshape(part.shape[:-1] + (width,))
        pieces.append(block[..., : part.shape[-1]])
        offset += count
    return tuple(pieces)


def allsum_large(values):
    n = lax.axis_size("dp")
    if n & (n - 1):
        return lax.psum(values, ("dp", "spatial"))
    me = lax.axis_index("dp")
    bits = []
    step = 1
    while step < n:
        bits.append(step)
        step *= 2
    for step in bits:
        half = values.shape[0] // 2
        high = (me // step) % 2
        keep = lax.dynamic_slice_in_dim(values, high * half, half, axis=0)
        send = lax.dynamic_slice_in_dim(values, (1 - high) * half, half, axis=0)
        values = keep + lax.ppermute(send, "dp", [(i, i ^ step) for i in range(n)])
    values = allsum_small(values, ("spatial",))
    for step in reversed(bits):
        high = (me // step) % 2
        other = lax.ppermute(values, "dp", [(i, i ^ step) for i in range(n)])
        values = jnp.where(
            high == 0,
            jnp.concatenate([values, other], axis=0),
            jnp.concatenate([other, values], axis=0),
        )
    return values


def solution(mesh):
    return jax.shard_map(
        local,
        mesh=mesh,
        in_specs=(
            P("dp", "spatial", None, None),
            P(),
            P(),
            P(),
            P(),
            P(),
            P(),
            P("dp", "spatial", None, None),
        ),
        out_specs=(
            P("dp", "spatial", None, None),
            P("dp", "spatial", None, None),
            P(),
            P(),
            P(),
            P(),
            P(),
            P(),
        ),
        check_vma=False,
    )
```

```python
import math

import jax
import jax.numpy as jnp
from jax import lax
from jax.sharding import PartitionSpec as P


LAT = 64
LON = 128
BLOCKS = 8
BLOCK = 96


shrink_cut = 0.01
norm_epsilon = 1e-06
gelu_factor = 0.7978845608
gelu_cubic = 0.044715


def product(pattern, left_side, right_side):
    return jnp.einsum(pattern, left_side, right_side, preferred_element_type=jnp.float32)


def tables(count, mode_count, doubled):
    positions = jnp.arange(count, dtype=jnp.int32)
    orders = jnp.arange(mode_count, dtype=jnp.int32)
    phases = orders[:, None] * positions[None, :] % count
    angles = 2.0 * math.pi / count * phases.astype(jnp.float32)
    factor = jnp.ones((mode_count, 1), jnp.float32) / math.sqrt(count)
    if doubled:
        factor = factor * jnp.where(orders == 0, 1.0, 2.0).astype(jnp.float32)[:, None]
    return (
        (jnp.cos(angles) * factor).astype(jnp.bfloat16),
        (jnp.sin(angles) * factor).astype(jnp.bfloat16),
    )


def rotate(values):
    half_width = values.shape[-1] // 2
    return jnp.concatenate([values[..., half_width:], -values[..., :half_width]], axis=-1)


def along_lon(real_part, cos_table, sin_table):
    real_sum = product("bhwnp,mw->bhmnp", real_part, cos_table)
    imag_sum = -product("bhwnp,mw->bhmnp", real_part, sin_table)
    return jnp.concatenate([real_sum, imag_sum], axis=-1).astype(jnp.bfloat16)


def back_lon(spectral, cos_table, sin_table):
    half_width = spectral.shape[-1] // 2
    return product("bhmnp,mw->bhwnp", spectral[..., :half_width], cos_table) - product(
        "bhmnp,mw->bhwnp", spectral[..., half_width:], sin_table
    )


def along_lat(spectral, cos_table, sin_table):
    stacked = jnp.concatenate([spectral, rotate(spectral)], axis=1)
    table = jnp.concatenate([cos_table, sin_table], axis=1)
    return product("kh,bhmnp->bkmnp", table, stacked).astype(jnp.bfloat16)


def back_lat(spectral, cos_table, sin_table):
    stacked = jnp.concatenate([spectral, -rotate(spectral)], axis=1)
    table = jnp.concatenate([cos_table, sin_table], axis=1)
    return product("kh,bhmnp->bkmnp", table, stacked).astype(jnp.bfloat16)


def real_blocks(weight):
    upper_rows = jnp.concatenate([weight[0], weight[1]], axis=-1)
    bottom = jnp.concatenate([-weight[1], weight[0]], axis=-1)
    return jnp.concatenate([upper_rows, bottom], axis=1)


def fold_blocks(gradient):
    half_width = gradient.shape[-1] // 2
    real_grad = gradient[:, :half_width, :half_width] + gradient[:, half_width:, half_width:]
    imag_grad = gradient[:, :half_width, half_width:] - gradient[:, half_width:, :half_width]
    return jnp.stack([real_grad, imag_grad])


def gelu_value(values):
    inner = jnp.tanh(gelu_factor * (values + gelu_cubic * values * values * values))
    return 0.5 * values * (1.0 + inner)


def gelu_slope(values):
    inner = jnp.tanh(gelu_factor * (values + gelu_cubic * values * values * values))
    return 0.5 * (1.0 + inner) + 0.5 * values * (1.0 - inner * inner) * gelu_factor * (
        1.0 + 3.0 * gelu_cubic * values * values
    )


def spectral_forward(transformed, first_real, first_bias, second_real, second_bias):
    hidden_pre = product("bkmnp,npq->bkmnq", transformed, first_real) + first_bias
    hidden = gelu_value(hidden_pre).astype(jnp.bfloat16)
    output_pre = product("bkmnp,npq->bkmnq", hidden, second_real) + second_bias
    shrunk = (output_pre - shrink_cut * jnp.tanh(output_pre / shrink_cut)).astype(jnp.bfloat16)
    return (hidden_pre, hidden, output_pre, shrunk)


def spectral_backward(
    transformed, hidden_pre, hidden, output_pre, grad_shrunk, first_real, second_real
):
    bend = jnp.tanh(output_pre / shrink_cut)
    grad_outpre = (grad_shrunk.astype(jnp.float32) * bend * bend).astype(jnp.bfloat16)
    grad_second = product("bkmnp,bkmnq->npq", hidden, grad_outpre)
    grad_second_bias = jnp.sum(grad_outpre.astype(jnp.float32), axis=(0, 1, 2))
    grad_hidden = product("bkmnq,npq->bkmnp", grad_outpre, second_real)
    grad_hidpre = (grad_hidden * gelu_slope(hidden_pre)).astype(jnp.bfloat16)
    grad_first = product("bkmnp,bkmnq->npq", transformed, grad_hidpre)
    grad_first_bias = jnp.sum(grad_hidpre.astype(jnp.float32), axis=(0, 1, 2))
    grad_transformed = product("bkmnq,npq->bkmnp", grad_hidpre, first_real).astype(jnp.bfloat16)
    return (grad_transformed, grad_first, grad_first_bias, grad_second, grad_second_bias)


def normalize(fields):
    values = fields.astype(jnp.float32)
    center = jnp.mean(values, axis=-1, keepdims=True)
    spread = jnp.mean((values - center) ** 2, axis=-1, keepdims=True)
    inverse_std = lax.rsqrt(spread + norm_epsilon)
    return ((values - center) * inverse_std, inverse_std)


def norm_backward(grad_scaled, normed, inverse_std, norm_gain):
    grad_normed = grad_scaled * norm_gain
    mean_grad = jnp.mean(grad_normed, axis=-1, keepdims=True)
    mean_cross = jnp.mean(grad_normed * normed, axis=-1, keepdims=True)
    return inverse_std * (grad_normed - mean_grad - normed * mean_cross)


def send_order(me, n, size):
    chunk = (me + jnp.arange(n, dtype=jnp.int32)[:, None]) % n
    return (chunk * size + jnp.arange(size, dtype=jnp.int32)[None, :]).reshape(-1)


def receive_order(me, n, size):
    chunk = (me + n - jnp.arange(n, dtype=jnp.int32)[:, None]) % n
    return (chunk * size + jnp.arange(size, dtype=jnp.int32)[None, :]).reshape(-1)


def exchange(values, split_axis, concat_axis):
    n = lax.axis_size("spatial")
    size = values.shape[split_axis] // n
    pieces = [lax.slice_in_dim(values, k * size, (k + 1) * size, axis=split_axis) for k in range(n)]
    received = [pieces[0]] + [
        lax.ppermute(pieces[k], "spatial", [(i, (i + k) % n) for i in range(n)])
        for k in range(1, n)
    ]
    return jnp.concatenate(received, axis=concat_axis)


def allsum_small(values, axes=("spatial", "dp")):
    for axis in axes:
        n = lax.axis_size(axis)
        if n & (n - 1):
            values = lax.psum(values, axis)
            continue
        step = 1
        while step < n:
            values = values + lax.ppermute(values, axis, [(i, i ^ step) for i in range(n)])
            step *= 2
    return values


def local(
    fields, norm_gain, norm_shift, first_weight, first_bias, second_weight, second_bias, cotangent
):
  samples, band_rows, longitudes, _ = fields.shape
  mode_count = longitudes // 2
  n = lax.axis_size("spatial")
  me = lax.axis_index("spatial")
  modes_per = mode_count // n
  send_m = send_order(me, n, modes_per)
  recv_m = receive_order(me, n, modes_per)
  send_h = send_order(me, n, band_rows)
  recv_h = receive_order(me, n, band_rows)
  ahead_cos, ahead_sin = tables(longitudes, mode_count, False)
  back_cos, back_sin = tables(longitudes, mode_count, True)
  polar_cos, polar_sin = tables(LAT, LAT, False)
  first_real = real_blocks(first_weight)
  second_real = real_blocks(second_weight)
  block_shape = (samples, band_rows, longitudes, BLOCKS, BLOCK)
  normed, inverse_std = normalize(fields)
  scaled = (normed * norm_gain + norm_shift).astype(jnp.bfloat16)
  spectral = along_lon(scaled.reshape(block_shape), ahead_cos[send_m], ahead_sin[send_m])
  columns = exchange(spectral, 2, 1)
  grad_returned = along_lon(cotangent.reshape(block_shape), back_cos[send_m], back_sin[send_m])
  grad_columns = exchange(grad_returned, 2, 1)
  transformed = along_lat(columns, polar_cos[:, recv_h], polar_sin[:, recv_h])
  hidden_pre, hidden, output_pre, shrunk = spectral_forward(
      transformed, first_real, first_bias, second_real, second_bias
  )
  returned = back_lat(shrunk, polar_cos[send_h], polar_sin[send_h])
  banded = exchange(returned, 1, 2)
  halves = []
  for lo, hi in ((0, BLOCKS // 2), (BLOCKS // 2, BLOCKS)):
      pick = lambda values: values[:, :, :, lo:hi]
      grad_shrunk = along_lat(pick(grad_columns), polar_cos[:, recv_h], polar_sin[:, recv_h])
      grad_transformed, g_first, g_first_bias, g_second, g_second_bias = spectral_backward(
          pick(transformed),
          pick(hidden_pre),
          pick(hidden),
          pick(output_pre),
          grad_shrunk,
          first_real[lo:hi],
          second_real[lo:hi],
      )
      grad_spectral = back_lat(grad_transformed, polar_cos[send_h], polar_sin[send_h])
      grad_banded = exchange(grad_spectral, 1, 2)
      halves.append((grad_banded, g_first, g_first_bias, g_second, g_second_bias))
  grad_banded, g_first, g_first_bias, g_second, g_second_bias = (
      jnp.concatenate(parts, axis=axis) for parts, axis in zip(zip(*halves), (3, 0, 0, 0, 0))
  )
  early = psum_flat((fold_blocks(g_first), g_first_bias, fold_blocks(g_second), g_second_bias))
  mixed = back_lon(banded, back_cos[recv_m], back_sin[recv_m]).reshape(fields.shape)
  block_output = (fields.astype(jnp.float32) + scaled.astype(jnp.float32) + mixed).astype(
      jnp.bfloat16
  )
  grad_scaled = cotangent.astype(jnp.float32) + back_lon(
      grad_banded, ahead_cos[recv_m], ahead_sin[recv_m]
  ).reshape(fields.shape)
  grad_fields = (
      cotangent.astype(jnp.float32) + norm_backward(grad_scaled, normed, inverse_std, norm_gain)
  ).astype(jnp.bfloat16)
  g_gain = jnp.sum(grad_scaled * normed, axis=(0, 1, 2))
  g_shift = jnp.sum(grad_scaled, axis=(0, 1, 2))
  late = allsum_small(jnp.stack([g_gain, g_shift]))
  token_total = lax.axis_size("dp") * samples * LAT * LON
  scale = 1.0 / math.sqrt(token_total)
  return (block_output, grad_fields) + tuple(part * scale for part in early) + (
      late[0] * scale,
      late[1] * scale,
  )


def psum_flat(parts):
    flat = jnp.concatenate([part.reshape(-1) for part in parts])
    size = flat.shape[0]
    unit = 1024 * lax.axis_size("dp")
    padded = -(-size // unit) * unit
    flat = jnp.pad(flat, (0, padded - size)).reshape(padded // 128, 128)
    flat = allsum_large(flat).reshape(-1)
    pieces, offset = [], 0
    for part in parts:
        pieces.append(flat[offset : offset + part.size].reshape(part.shape))
        offset += part.size
    return tuple(pieces)


def allsum_large(values):
    n = lax.axis_size("dp")
    if n & (n - 1):
        return lax.psum(values, ("dp", "spatial"))
    me = lax.axis_index("dp")
    bits = []
    step = 1
    while step < n:
        bits.append(step)
        step *= 2
    for step in bits:
        half = values.shape[0] // 2
        high = (me // step) % 2
        keep = lax.dynamic_slice_in_dim(values, high * half, half, axis=0)
        send = lax.dynamic_slice_in_dim(values, (1 - high) * half, half, axis=0)
        sent = lax.ppermute(send.astype(jnp.bfloat16), "dp", [(i, i ^ step) for i in range(n)])
        values = keep + sent.astype(jnp.float32)
    values = allsum_small(values, ("spatial",))
    for step in reversed(bits):
        high = (me // step) % 2
        values = values.astype(jnp.bfloat16).astype(jnp.float32)
        other = lax.ppermute(values.astype(jnp.bfloat16), "dp", [(i, i ^ step) for i in range(n)])
        other = other.astype(jnp.float32)
        values = jnp.where(
            high == 0,
            jnp.concatenate([values, other], axis=0),
            jnp.concatenate([other, values], axis=0),
        )
    return values


def solution(mesh):
    return jax.shard_map(
        local,
        mesh=mesh,
        in_specs=(
            P("dp", "spatial", None, None),
            P(),
            P(),
            P(),
            P(),
            P(),
            P(),
            P("dp", "spatial", None, None),
        ),
        out_specs=(
            P("dp", "spatial", None, None),
            P("dp", "spatial", None, None),
            P(),
            P(),
            P(),
            P(),
            P(),
            P(),
        ),
        check_vma=False,
    )
```
